128 devices in a mesh: req: 64 (over z, y, x_hi, core), tok: 2 (over x_lo).
Axes of the slice: x: 4 (x_hi: 2, x_lo: 2; x = x_hi * 2 + x_lo), y: 4, z: 4, core: 2. Of those that a mesh axis runs over, the one named last changes fastest.
Arguments:
- hidden_in: bfloat16 [128, 256, 2560], P('req', 'tok'), may hold values from -40 to 40
- cache_keys: bfloat16 [128, 4096, 320], P('req', None, 'tok'), may hold values from -100 to 100
- stored_cache_values: bfloat16 [128, 4096, 320], P('req', None, 'tok'), may hold values from -5 to 5
- cache_lengths: int32 [128], P('req'), may hold values from 0 to 16384, as said below
- live_slots: int32 [128], replicated, may hold values from 0 to 1, as said below
- attn_gain: float32 [2560], replicated, may hold values from 0.1 to 1.9
- w_query: bfloat16 [2560, 1280], P(None, 'tok'), may hold values from -0.125 to 0.125
- key_weight: bfloat16 [2560, 320], P(None, 'tok'), may hold values from -0.125 to 0.125
- value_weight: bfloat16 [2560, 320], P(None, 'tok'), may hold values from -0.125 to 0.125
- w_out: bfloat16 [1280, 2560], P('tok'), may hold values from -0.15625 to 0.15625
- mlp_gain: float32 [2560], replicated, may hold values from 0.1 to 1.9
- w_gate: bfloat16 [2560, 3584], P(None, 'tok'), may hold values from -0.125 to 0.125
- w_up: bfloat16 [2560, 3584], P(None, 'tok'), may hold values from -0.125 to 0.125
- w_down: bfloat16 [3584, 2560], P('tok'), may hold values from -0.09375 to 0.09375
Outputs:
- hidden_out: bfloat16 [128, 256, 2560], P('req', 'tok')
- new_keys: bfloat16 [128, 256, 320], P('req', None, 'tok')
- new_values: bfloat16 [128, 256, 320], P('req', None, 'tok')
The draws below stay inside these ranges and needn't reach their ends.
Inputs may be any that keep to these rules, and one draw needn't show every extreme that they name: `live_slots`: exactly 64 of the 128 slots are live; the 2 slots of one index of req hold 0, 1 or 2 live requests, and some index holds two. `cache_lengths`: 0 for a slot that is not live; some live slot has exactly 16384.
All inputs are finite; a program needn't handle non-finite values.
Results may differ from the reference program's by a relative error of at most 0.0095.
Values may be sent and summed in bfloat16 or wider, within the bound.
No kernel may reach another device: no remote copies, remote signals or barrier semaphores. Data moves between devices by JAX's collectives and lax.ppermute only.
A program may use at most 192 MiB of HBM per device.

```python
import jax
import jax.numpy as jnp
from jax import lax

MODEL_DIM = 2560
QUERY_HEADS = 16
KEY_VALUE_HEADS = 4
HEAD_DIM = 80
FFW = 3584
NEW_TOKENS = 256
WINDOW_POSITIONS = 4096
LMAX = 16384
ALL_REQUEST_SLOTS = 128
REQUESTS = 64


def plan_slots(key):
    base_key = jax.random.fold_in(key, 17)
    order_key, pick_key, length_key = jax.random.split(base_key, 3)
    order = jax.random.permutation(order_key, REQUESTS)
    ranks = jnp.zeros((REQUESTS,), jnp.int32).at[order].set(jnp.arange(REQUESTS, dtype=jnp.int32))
    quota = max(1, REQUESTS // 8)
    counts = jnp.where(ranks < quota, 2, jnp.where(ranks < 2 * quota, 0, 1))
    picks = jax.random.randint(pick_key, (REQUESTS,), 0, 2)
    first_slot = (counts == 2) | (counts == 1) & (picks == 0)
    second_slot = (counts == 2) | (counts == 1) & (picks == 1)
    alive = jnp.stack([first_slot, second_slot], axis=1).reshape(ALL_REQUEST_SLOTS).astype(jnp.int32)
    factors = jax.random.randint(length_key, (3, ALL_REQUEST_SLOTS), 0, LMAX + 1)
    lengths = factors[0] * factors[1] // LMAX * factors[2] // LMAX
    longest = jnp.repeat(ranks == 0, 2) & (jnp.arange(ALL_REQUEST_SLOTS) % 2 == 0)
    lengths = jnp.where(longest, LMAX, lengths)
    return (alive, (lengths * alive).astype(jnp.int32))


def draw_live_slots(key, part):
    return plan_slots(key)[0]


def draw_cache_lengths(key, part):
    return plan_slots(key)[1]


def draw_hidden_in(key, part):
    row_key, column_key, base_key = jax.random.split(jax.random.fold_in(key, 29), 3)
    target_shape = (ALL_REQUEST_SLOTS, NEW_TOKENS, MODEL_DIM)
    row_scale = jnp.exp(jax.random.uniform(row_key, (ALL_REQUEST_SLOTS, NEW_TOKENS, 1), jnp.float32, -1.15, 1.15))
    column_scale = jnp.exp(jax.random.uniform(column_key, (1, 1, MODEL_DIM), jnp.float32, -1.15, 1.15))
    starting_offset = jnp.clip(jax.random.normal(base_key, target_shape, jnp.float32), -4.0, 4.0)
    return (starting_offset * row_scale * column_scale).astype(jnp.bfloat16)


def draw_cache_keys(key, part):
    collected_keys = jax.random.split(jax.random.fold_in(key, 41), 6)
    target_shape = (ALL_REQUEST_SLOTS, WINDOW_POSITIONS, KEY_VALUE_HEADS * HEAD_DIM)
    nearby_boundary = min(NEW_TOKENS, WINDOW_POSITIONS // 4)
    distant_boundary = WINDOW_POSITIONS // 2
    surge_width = min(32, WINDOW_POSITIONS // 8)
    slot_position = jnp.arange(WINDOW_POSITIONS)[None, :, None]
    surge_position = jax.random.randint(collected_keys[5], (ALL_REQUEST_SLOTS, 1, 1), nearby_boundary, distant_boundary - surge_width)
    inside_surge = (slot_position >= surge_position) & (slot_position < surge_position + surge_width)
    final_output = jnp.clip(jax.random.normal(collected_keys[0], target_shape, jnp.float32), -4.0, 4.0)
    final_output = jnp.where(inside_surge, 4.0 * final_output, final_output)
    return final_output.astype(jnp.bfloat16)


def levels(own_key, extent, cuts, low, top_value):
    level, own = 1.0, jax.random.fold_in(own_key, 6)
    for position, shards_of in cuts:
        draws = jnp.exp(jax.random.uniform(jax.random.fold_in(own, position), (shards_of,), jnp.float32, low / len(cuts), top_value / len(cuts)))
        level = level * jnp.repeat(draws, extent[position] // shards_of).reshape([-1 if axis == position else 1 for axis in range(len(extent))])
    return level


def centred(rng, shape, scale, most, cuts=(), kind=jnp.bfloat16):
    gain = levels(rng, shape, cuts, -0.22, 0.18) if cuts else 1.0
    result = jax.random.normal(rng, shape, jnp.float32) * scale * gain
    return jnp.minimum(jnp.maximum(result, -most), most).astype(kind)


def setup_inputs(seed: int = 0) -> dict:
    arg_keys = jax.random.split(jax.random.key(seed), 15)
    hidden_in = draw_hidden_in(jax.random.fold_in(arg_keys[14], 71), 0)
    cache_keys = draw_cache_keys(jax.random.fold_in(arg_keys[14], 71), 0)
    stored_cache_values = centred(arg_keys[2], (ALL_REQUEST_SLOTS, WINDOW_POSITIONS, KEY_VALUE_HEADS * HEAD_DIM), 1.0, 5.0, ((0, 64), (2, 2)))
    cache_lengths = draw_cache_lengths(jax.random.fold_in(arg_keys[14], 71), 0)
    live_slots = draw_live_slots(jax.random.fold_in(arg_keys[14], 71), 0)
    attn_gain = jnp.clip(1.0 + 0.18 * jax.random.normal(arg_keys[5], (MODEL_DIM,), jnp.float32), 0.1, 1.9)
    w_query = centred(arg_keys[6], (MODEL_DIM, QUERY_HEADS * HEAD_DIM), MODEL_DIM ** -0.5, 0.125, ((1, 2),))
    key_weight = centred(arg_keys[7], (MODEL_DIM, KEY_VALUE_HEADS * HEAD_DIM), MODEL_DIM ** -0.5, 0.125, ((1, 2),))
    value_weight = centred(arg_keys[8], (MODEL_DIM, KEY_VALUE_HEADS * HEAD_DIM), MODEL_DIM ** -0.5, 0.125, ((1, 2),))
    w_out = centred(arg_keys[9], (QUERY_HEADS * HEAD_DIM, MODEL_DIM), (QUERY_HEADS * HEAD_DIM) ** -0.5, 0.15625, ((0, 2),))
    mlp_gain = jnp.clip(1.0 + 0.18 * jax.random.normal(arg_keys[10], (MODEL_DIM,), jnp.float32), 0.1, 1.9)
    w_gate = centred(arg_keys[11], (MODEL_DIM, FFW), MODEL_DIM ** -0.5, 0.125, ((1, 2),))
    w_up = centred(arg_keys[12], (MODEL_DIM, FFW), MODEL_DIM ** -0.5, 0.125, ((1, 2),))
    w_down = centred(arg_keys[13], (FFW, MODEL_DIM), FFW ** -0.5, 0.09375, ((0, 2),))
    return dict(hidden_in=hidden_in, cache_keys=cache_keys, stored_cache_values=stored_cache_values, cache_lengths=cache_lengths, live_slots=live_slots, attn_gain=attn_gain, w_query=w_query, key_weight=key_weight, value_weight=value_weight, w_out=w_out, mlp_gain=mlp_gain, w_gate=w_gate, w_up=w_up, w_down=w_down)


EPSILON = 1e-05
ROPE_BASE = 10000.0

def rms_norm(values, norm_gain):
    widened = values.astype(jnp.float32)
    mean_square = lax.optimization_barrier(jnp.mean(widened * widened, axis=-1, keepdims=True))
    return widened * lax.rsqrt(mean_square + EPSILON) * norm_gain

def apply_rotary(values, token_positions):
    full_width = values.shape[-1]
    half_width = full_width // 2
    inverse = ROPE_BASE ** (-(jnp.arange(half_width, dtype=jnp.float32) * 2.0) / full_width)
    angles = token_positions.astype(jnp.float32)[..., None] * inverse
    cosine = jnp.cos(angles)[..., None, :]
    sine_part = jnp.sin(angles)[..., None, :]
    first_half = values[..., :half_width]
    second_half = values[..., half_width:]
    return jnp.concatenate([first_half * cosine - second_half * sine_part, second_half * cosine + first_half * sine_part], axis=-1)

def reference(hidden_in, cache_keys, stored_cache_values, cache_lengths, live_slots, attn_gain, w_query, key_weight, value_weight, w_out, mlp_gain, w_gate, w_up, w_down):
    query_group_count = QUERY_HEADS // KEY_VALUE_HEADS
    scaling = HEAD_DIM ** (-0.5)

    def one_slot(slot_items):
        tokens, cached_keys, cached_values, length, alive = slot_items
        normed = rms_norm(tokens, attn_gain).astype(jnp.bfloat16)
        queries = jnp.dot(normed, w_query, preferred_element_type=jnp.float32)
        incoming_keys = jnp.dot(normed, key_weight, preferred_element_type=jnp.float32)
        incoming_values = jnp.dot(normed, value_weight, preferred_element_type=jnp.float32)
        token_positions = length + jnp.arange(NEW_TOKENS, dtype=jnp.int32)
        queries = apply_rotary(queries.reshape(NEW_TOKENS, QUERY_HEADS, HEAD_DIM), token_positions).astype(jnp.bfloat16)
        incoming_keys = apply_rotary(incoming_keys.reshape(NEW_TOKENS, KEY_VALUE_HEADS, HEAD_DIM), token_positions).astype(jnp.bfloat16)
        incoming_values = incoming_values.astype(jnp.bfloat16).reshape(NEW_TOKENS, KEY_VALUE_HEADS, HEAD_DIM)
        key_pos = jnp.concatenate([length - WINDOW_POSITIONS + jnp.arange(WINDOW_POSITIONS, dtype=jnp.int32), token_positions])
        visible = (key_pos[None, :] >= 0) & (key_pos[None, :] <= token_positions[:, None]) & (token_positions[:, None] - key_pos[None, :] < WINDOW_POSITIONS)
        head_results = []
        for current_head_index in range(KEY_VALUE_HEADS):
            all_keys = jnp.concatenate([cached_keys[:, current_head_index * HEAD_DIM:(current_head_index + 1) * HEAD_DIM], incoming_keys[:, current_head_index, :]], axis=0)
            all_values = jnp.concatenate([cached_values[:, current_head_index * HEAD_DIM:(current_head_index + 1) * HEAD_DIM], incoming_values[:, current_head_index, :]], axis=0)
            head_queries = queries[:, current_head_index * query_group_count:(current_head_index + 1) * query_group_count, :]
            scores = jnp.einsum('tgd,ud->tgu', head_queries.astype(jnp.float32), all_keys.astype(jnp.float32)) * scaling
            scores = jnp.where(visible[:, None, :], scores, -jnp.inf)
            top = lax.optimization_barrier(jnp.max(scores, axis=-1, keepdims=True))
            raised = jnp.exp(scores - top)
            mass = lax.optimization_barrier(jnp.sum(raised, axis=-1, keepdims=True))
            weights = (raised / mass).astype(jnp.bfloat16)
            head_results.append(jnp.einsum('tgu,ud->tgd', weights.astype(jnp.float32), all_values.astype(jnp.float32)))
        attended = jnp.stack(head_results, axis=1).reshape(NEW_TOKENS, QUERY_HEADS * HEAD_DIM).astype(jnp.bfloat16)
        residual = (tokens.astype(jnp.float32) + jnp.dot(attended, w_out, preferred_element_type=jnp.float32)).astype(jnp.bfloat16)
        mlp_in = rms_norm(residual, mlp_gain).astype(jnp.bfloat16)
        gate_part = jnp.dot(mlp_in, w_gate, preferred_element_type=jnp.float32)
        up_part = jnp.dot(mlp_in, w_up, preferred_element_type=jnp.float32)
        activated = (jax.nn.silu(gate_part) * up_part).astype(jnp.bfloat16)
        completed_output = (residual.astype(jnp.float32) + jnp.dot(activated, w_down, preferred_element_type=jnp.float32)).astype(jnp.bfloat16)
        window_mask = alive > 0
        empty_value_rows = jnp.zeros((), jnp.bfloat16)
        return (jnp.where(window_mask, completed_output, empty_value_rows), jnp.where(window_mask, incoming_keys.reshape(NEW_TOKENS, KEY_VALUE_HEADS * HEAD_DIM), empty_value_rows), jnp.where(window_mask, incoming_values.reshape(NEW_TOKENS, KEY_VALUE_HEADS * HEAD_DIM), empty_value_rows))
    hidden_out, new_keys, new_values = lax.map(one_slot, (hidden_in, cache_keys, stored_cache_values, cache_lengths, live_slots))
    return (hidden_out, new_keys, new_values)
```

```python
import functools

import jax
import jax.numpy as jnp
from jax import lax
from jax.experimental import pallas as pl
from jax.experimental.pallas import tpu as pltpu
from jax.sharding import PartitionSpec as P

HEAD_DIM = 80


EPSILON = 1e-05
ROPE_BASE = 10000.0


def rms_norm(values, norm_gain):
    widened = values.astype(jnp.float32)
    mean_square = jnp.mean(widened * widened, axis=-1, keepdims=True)
    return widened * lax.rsqrt(mean_square + EPSILON) * norm_gain


def apply_rotary(values, token_positions):
    full_width = values.shape[-1]
    half_width = full_width // 2
    inverse = ROPE_BASE ** (-(jnp.arange(half_width, dtype=jnp.float32) * 2.0) / full_width)
    angles = token_positions.astype(jnp.float32)[..., None] * inverse
    cosine = jnp.cos(angles)[..., None, :]
    sine_part = jnp.sin(angles)[..., None, :]
    first_half = values[..., :half_width]
    second_half = values[..., half_width:]
    return jnp.concatenate(
        [
            first_half * cosine - second_half * sine_part,
            second_half * cosine + first_half * sine_part,
        ],
        axis=-1,
    )


NEG = -jnp.inf
KEY_BLOCK = 512


def attention_kernel(len_ref, q_ref, kc_ref, vc_ref, kn_ref, vn_ref, o_ref, *, group, scaling):
    slot = pl.program_id(0)
    rows = q_ref.shape[1]
    window = kc_ref.shape[1]
    fresh = kn_ref.shape[1]
    heads_rows = fresh * group
    length = len_ref[slot]
    q = q_ref[0]
    row = pl.program_id(1) * rows + lax.broadcasted_iota(jnp.int32, (rows, 1), 0)
    token = (row % heads_rows) // group
    dims = (((1,), (1,)), ((), ()))
    scores = lax.dot_general(q, kn_ref[0], dims, preferred_element_type=jnp.float32) * scaling
    fresh_pos = lax.broadcasted_iota(jnp.int32, (1, fresh), 1)
    scores = jnp.where(fresh_pos <= token, scores, NEG)
    top = jnp.max(scores, axis=1, keepdims=True)
    raised = jnp.exp(scores - top)
    mass = jnp.sum(raised, axis=1, keepdims=True)
    total = jnp.dot(raised.astype(jnp.bfloat16), vn_ref[0], preferred_element_type=jnp.float32)
    lowest = window - length
    first_block = jnp.maximum(lowest, 0) // KEY_BLOCK

    def body(block, carry):
        top, mass, total = carry
        begin = pl.multiple_of(block * KEY_BLOCK, KEY_BLOCK)
        keys = kc_ref[0, pl.ds(begin, KEY_BLOCK), :]
        values = vc_ref[0, pl.ds(begin, KEY_BLOCK), :]
        scores = lax.dot_general(q, keys, dims, preferred_element_type=jnp.float32) * scaling
        key_pos = begin + lax.broadcasted_iota(jnp.int32, (1, KEY_BLOCK), 1)
        visible = (key_pos >= lowest) & (key_pos > token)
        scores = jnp.where(visible, scores, NEG)
        raised_top = jnp.maximum(top, jnp.max(scores, axis=1, keepdims=True))
        shrink = jnp.exp(top - raised_top)
        raised = jnp.exp(scores - raised_top)
        mass = mass * shrink + jnp.sum(raised, axis=1, keepdims=True)
        total = total * shrink + jnp.dot(
            raised.astype(jnp.bfloat16), values, preferred_element_type=jnp.float32
        )
        return raised_top, mass, total

    top, mass, total = lax.fori_loop(first_block, window // KEY_BLOCK, body, (top, mass, total))
    o_ref[0] = (total / mass).astype(o_ref.dtype)


def attend_all(padded_queries, cache_keys, cache_values, fresh_keys, fresh_values, lengths, group):
    slots, total_rows, width = padded_queries.shape
    window = cache_keys.shape[1]
    fresh = fresh_keys.shape[1]
    rows = 512
    scaling = HEAD_DIM ** (-0.5)
    kernel = functools.partial(attention_kernel, group=group, scaling=scaling)
    flops = 2 * 2 * slots * total_rows * (window + fresh) * width
    cost = pl.CostEstimate(
        flops=flops,
        transcendentals=slots * total_rows * (window + fresh),
        bytes_accessed=2 * (2 * padded_queries.size + 2 * cache_keys.size + 2 * fresh_keys.size),
    )
    return pl.pallas_call(
        kernel,
        grid_spec=pltpu.PrefetchScalarGridSpec(
            num_scalar_prefetch=1,
            grid=(slots, total_rows // rows),
            in_specs=[
                pl.BlockSpec((1, rows, width), lambda s, r, n: (s, r, 0)),
                pl.BlockSpec((1, window, width), lambda s, r, n: (s, 0, 0)),
                pl.BlockSpec((1, window, width), lambda s, r, n: (s, 0, 0)),
                pl.BlockSpec((1, fresh, width), lambda s, r, n: (s, 0, 0)),
                pl.BlockSpec((1, fresh, width), lambda s, r, n: (s, 0, 0)),
            ],
            out_specs=pl.BlockSpec((1, rows, width), lambda s, r, n: (s, r, 0)),
        ),
        out_shape=jax.ShapeDtypeStruct((slots, total_rows, width), jnp.bfloat16),
        compiler_params=pltpu.CompilerParams(dimension_semantics=("arbitrary", "arbitrary")),
        cost_estimate=cost,
    )(lengths, padded_queries, cache_keys, cache_values, fresh_keys, fresh_values)


def feed_forward(rows_in, mlp_gain, w_gate, w_up, w_down):
    normed_rows = rms_norm(rows_in, mlp_gain).astype(jnp.bfloat16)
    block_rows = lax.all_gather(normed_rows, "tok", axis=0, tiled=True)
    gate_part = jnp.dot(block_rows, w_gate, preferred_element_type=jnp.float32)
    up_part = jnp.dot(block_rows, w_up, preferred_element_type=jnp.float32)
    activated = (jax.nn.silu(gate_part) * up_part).astype(jnp.bfloat16)
    summed = lax.psum_scatter(
        jnp.dot(
            lax.slice_in_dim(activated, 0, rows_in.shape[0] * lax.axis_size("tok"), axis=0),
            w_down,
            preferred_element_type=jnp.float32,
        ).astype(jnp.bfloat16),
        "tok",
        scatter_dimension=0,
        tiled=True,
    ).astype(jnp.float32)
    return (rows_in.astype(jnp.float32) + summed).astype(jnp.bfloat16)


def local(
    hidden_in,
    cache_keys,
    stored_cache_values,
    cache_lengths,
    live_slots,
    attn_gain,
    w_query,
    key_weight,
    value_weight,
    w_out,
    mlp_gain,
    w_gate,
    w_up,
    w_down,
):
    slots, quarter, model_width = hidden_in.shape
    new_rows = quarter * lax.axis_size("tok")
    query_width = w_query.shape[1]
    key_width = key_weight.shape[1]
    query_heads = query_width // HEAD_DIM
    key_heads = key_width // HEAD_DIM
    query_group_count = query_heads // key_heads
    alive_slots = lax.dynamic_slice_in_dim(live_slots, lax.axis_index("req") * slots, slots)
    window_mask = alive_slots[:, None, None] > 0
    empty_value_rows = jnp.zeros((), jnp.bfloat16)
    normed = rms_norm(hidden_in, attn_gain).astype(jnp.bfloat16)
    block_rows = lax.all_gather(normed, "tok", axis=1, tiled=True)
    mixed_rows = jnp.concatenate(
        [
            jnp.einsum("srd,dh->srh", block_rows, matrix, preferred_element_type=jnp.float32)
            for matrix in (w_query, key_weight, value_weight)
        ],
        axis=2,
    )
    token_positions = cache_lengths[:, None] + jnp.arange(new_rows, dtype=jnp.int32)[None, :]
    queries = apply_rotary(
        mixed_rows[..., :query_width].reshape(slots, new_rows, query_heads, HEAD_DIM),
        token_positions,
    ).astype(jnp.bfloat16)
    incoming_keys = apply_rotary(
        mixed_rows[..., query_width : query_width + key_width].reshape(
            slots, new_rows, key_heads, HEAD_DIM
        ),
        token_positions,
    ).astype(jnp.bfloat16)
    incoming_values = (
        mixed_rows[..., query_width + key_width :]
        .astype(jnp.bfloat16)
        .reshape(slots, new_rows, key_heads, HEAD_DIM)
    )
    new_keys = jnp.where(
        window_mask, incoming_keys.reshape(slots, new_rows, key_width), empty_value_rows
    )
    new_values = jnp.where(
        window_mask, incoming_values.reshape(slots, new_rows, key_width), empty_value_rows
    )
    padded = []
    for current_head_index in range(key_heads):
        head_queries = queries[
            :, :, current_head_index * query_group_count : (current_head_index + 1) * query_group_count, :
        ].reshape(slots, new_rows * query_group_count, HEAD_DIM)
        padded.append(
            jnp.pad(
                head_queries,
                ((0, 0), (0, 0), (current_head_index * HEAD_DIM, (key_heads - 1 - current_head_index) * HEAD_DIM)),
            )
        )
    attended_rows = attend_all(
        jnp.concatenate(padded, axis=1),
        cache_keys,
        stored_cache_values,
        incoming_keys.reshape(slots, new_rows, key_width),
        incoming_values.reshape(slots, new_rows, key_width),
        cache_lengths,
        query_group_count,
    )
    head_rows = new_rows * query_group_count
    attended = jnp.concatenate(
        [
            attended_rows[
                :, h * head_rows : (h + 1) * head_rows, h * HEAD_DIM : (h + 1) * HEAD_DIM
            ].reshape(slots, new_rows, query_group_count * HEAD_DIM)
            for h in range(key_heads)
        ],
        axis=2,
    )
    block_rows = attended
    projected = lax.psum_scatter(
        jnp.einsum("sth,hd->tsd", block_rows, w_out, preferred_element_type=jnp.float32).astype(
            jnp.bfloat16
        ),
        "tok",
        scatter_dimension=0,
        tiled=True,
    ).astype(jnp.float32)
    projected = jnp.transpose(projected, (1, 0, 2))
    residual = (hidden_in.astype(jnp.float32) + projected).astype(jnp.bfloat16)
    spread_rows = lax.all_to_all(residual, "req", split_axis=1, concat_axis=0, tiled=True)
    picked_index = jnp.nonzero(live_slots > 0, size=lax.axis_size("req"), fill_value=0)[0].astype(
        jnp.int32
    )
    picked = jnp.take(spread_rows, picked_index, axis=0)
    completed_output = feed_forward(
        picked.reshape(-1, model_width), mlp_gain, w_gate, w_up, w_down
    ).reshape(picked.shape)
    placed = jnp.zeros_like(spread_rows).at[picked_index].set(completed_output)
    hidden_out = lax.all_to_all(placed, "req", split_axis=0, concat_axis=1, tiled=True)
    return (hidden_out, new_keys, new_values)


def solution(mesh):
    return jax.shard_map(
        local,
        mesh=mesh,
        in_specs=(
            P("req", "tok", None),
            P("req", None, "tok"),
            P("req", None, "tok"),
            P("req"),
            P(),
            P(),
            P(None, "tok"),
            P(None, "tok"),
            P(None, "tok"),
            P("tok", None),
            P(),
            P(None, "tok"),
            P(None, "tok"),
            P("tok", None),
        ),
        out_specs=(P("req", "tok", None), P("req", None, "tok"), P("req", None, "tok")),
        check_vma=False,
    )
```

```python
import functools

import jax
import jax.numpy as jnp
from jax import lax
from jax.experimental import pallas as pl
from jax.experimental.pallas import tpu as pltpu
from jax.sharding import PartitionSpec as P

HEAD_DIM = 80


EPSILON = 1e-05
ROPE_BASE = 10000.0


def rms_norm(values, norm_gain):
    widened = values.astype(jnp.float32)
    mean_square = jnp.mean(widened * widened, axis=-1, keepdims=True)
    return widened * lax.rsqrt(mean_square + EPSILON) * norm_gain


def tok_gather(part, axis):
    me = lax.axis_index("tok")
    other = lax.ppermute(part, "tok", [(0, 1), (1, 0)])
    first = jnp.where(me == 0, part, other)
    second = jnp.where(me == 0, other, part)
    return jnp.concatenate([first, second], axis=axis)


def tok_reduce(whole, axis):
    me = lax.axis_index("tok")
    half = whole.shape[axis] // 2
    low = lax.slice_in_dim(whole, 0, half, axis=axis)
    high = lax.slice_in_dim(whole, half, 2 * half, axis=axis)
    keep = jnp.where(me == 0, low, high)
    send = jnp.where(me == 0, high, low).astype(jnp.bfloat16)
    other = lax.ppermute(send, "tok", [(0, 1), (1, 0)])
    return keep + other.astype(jnp.float32)


def apply_rotary(values, token_positions):
    full_width = values.shape[-1]
    half_width = full_width // 2
    inverse = ROPE_BASE ** (-(jnp.arange(half_width, dtype=jnp.float32) * 2.0) / full_width)
    angles = token_positions.astype(jnp.float32)[..., None] * inverse
    cosine = jnp.cos(angles)[..., None, :]
    sine_part = jnp.sin(angles)[..., None, :]
    first_half = values[..., :half_width]
    second_half = values[..., half_width:]
    return jnp.concatenate(
        [
            first_half * cosine - second_half * sine_part,
            second_half * cosine + first_half * sine_part,
        ],
        axis=-1,
    )


NEG = -jnp.inf
KEY_BLOCK = 512


def attention_kernel(len_ref, q_ref, kc_ref, vc_ref, kn_ref, vn_ref, o_ref, *, group, scaling):
    slot = pl.program_id(0)
    rows = q_ref.shape[1]
    window = kc_ref.shape[1]
    fresh = kn_ref.shape[1]
    heads_rows = fresh * group
    length = len_ref[slot]
    q = q_ref[0]
    row = pl.program_id(1) * rows + lax.broadcasted_iota(jnp.int32, (rows, 1), 0)
    token = (row % heads_rows) // group
    dims = (((1,), (1,)), ((), ()))
    scores = lax.dot_general(q, kn_ref[0], dims, preferred_element_type=jnp.float32) * scaling
    fresh_pos = lax.broadcasted_iota(jnp.int32, (1, fresh), 1)
    scores = jnp.where(fresh_pos <= token, scores, NEG)
    top = jnp.max(scores, axis=1, keepdims=True)
    raised = jnp.exp(scores - top)
    mass = jnp.sum(raised, axis=1, keepdims=True)
    total = jnp.dot(raised.astype(jnp.bfloat16), vn_ref[0], preferred_element_type=jnp.float32)
    lowest = window - length
    first_block = jnp.maximum(lowest, 0) // KEY_BLOCK

    def body(block, carry):
        top, mass, total = carry
        begin = pl.multiple_of(block * KEY_BLOCK, KEY_BLOCK)
        keys = kc_ref[0, pl.ds(begin, KEY_BLOCK), :]
        values = vc_ref[0, pl.ds(begin, KEY_BLOCK), :]
        scores = lax.dot_general(q, keys, dims, preferred_element_type=jnp.float32) * scaling
        key_pos = begin + lax.broadcasted_iota(jnp.int32, (1, KEY_BLOCK), 1)
        visible = (key_pos >= lowest) & (key_pos > token)
        scores = jnp.where(visible, scores, NEG)
        raised_top = jnp.maximum(top, jnp.max(scores, axis=1, keepdims=True))
        shrink = jnp.exp(top - raised_top)
        raised = jnp.exp(scores - raised_top)
        mass = mass * shrink + jnp.sum(raised, axis=1, keepdims=True)
        total = total * shrink + jnp.dot(
            raised.astype(jnp.bfloat16), values, preferred_element_type=jnp.float32
        )
        return raised_top, mass, total

    top, mass, total = lax.fori_loop(first_block, window // KEY_BLOCK, body, (top, mass, total))
    o_ref[0] = (total / mass).astype(o_ref.dtype)


def attend_all(padded_queries, cache_keys, cache_values, fresh_keys, fresh_values, lengths, group):
    slots, total_rows, width = padded_queries.shape
    window = cache_keys.shape[1]
    fresh = fresh_keys.shape[1]
    rows = 512
    scaling = HEAD_DIM ** (-0.5)
    kernel = functools.partial(attention_kernel, group=group, scaling=scaling)
    flops = 2 * 2 * slots * total_rows * (window + fresh) * width
    cost = pl.CostEstimate(
        flops=flops,
        transcendentals=slots * total_rows * (window + fresh),
        bytes_accessed=2 * (2 * padded_queries.size + 2 * cache_keys.size + 2 * fresh_keys.size),
    )
    return pl.pallas_call(
        kernel,
        grid_spec=pltpu.PrefetchScalarGridSpec(
            num_scalar_prefetch=1,
            grid=(slots, total_rows // rows),
            in_specs=[
                pl.BlockSpec((1, rows, width), lambda s, r, n: (s, r, 0)),
                pl.BlockSpec((1, window, width), lambda s, r, n: (s, 0, 0)),
                pl.BlockSpec((1, window, width), lambda s, r, n: (s, 0, 0)),
                pl.BlockSpec((1, fresh, width), lambda s, r, n: (s, 0, 0)),
                pl.BlockSpec((1, fresh, width), lambda s, r, n: (s, 0, 0)),
            ],
            out_specs=pl.BlockSpec((1, rows, width), lambda s, r, n: (s, r, 0)),
        ),
        out_shape=jax.ShapeDtypeStruct((slots, total_rows, width), jnp.bfloat16),
        compiler_params=pltpu.CompilerParams(dimension_semantics=("arbitrary", "arbitrary")),
        cost_estimate=cost,
    )(lengths, padded_queries, cache_keys, cache_values, fresh_keys, fresh_values)


def feed_forward(rows_in, mlp_gain, w_gate, w_up, w_down):
    normed_rows = rms_norm(rows_in, mlp_gain).astype(jnp.bfloat16)
    block_rows = tok_gather(normed_rows, 0)
    gate_part = jnp.dot(block_rows, w_gate, preferred_element_type=jnp.float32)
    up_part = jnp.dot(block_rows, w_up, preferred_element_type=jnp.float32)
    activated = (jax.nn.silu(gate_part) * up_part).astype(jnp.bfloat16)
    summed = tok_reduce(
        jnp.dot(activated, w_down, preferred_element_type=jnp.float32), 0
    )
    return (rows_in.astype(jnp.float32) + summed).astype(jnp.bfloat16)


def local(
    hidden_in,
    cache_keys,
    stored_cache_values,
    cache_lengths,
    live_slots,
    attn_gain,
    w_query,
    key_weight,
    value_weight,
    w_out,
    mlp_gain,
    w_gate,
    w_up,
    w_down,
):
    slots, quarter, model_width = hidden_in.shape
    new_rows = quarter * lax.axis_size("tok")
    query_width = w_query.shape[1]
    key_width = key_weight.shape[1]
    query_heads = query_width // HEAD_DIM
    key_heads = key_width // HEAD_DIM
    query_group_count = query_heads // key_heads
    alive_slots = lax.dynamic_slice_in_dim(live_slots, lax.axis_index("req") * slots, slots)
    window_mask = alive_slots[:, None, None] > 0
    empty_value_rows = jnp.zeros((), jnp.bfloat16)
    normed = rms_norm(hidden_in, attn_gain).astype(jnp.bfloat16)
    block_rows = tok_gather(normed, 1)
    mixed_rows = jnp.concatenate(
        [
            jnp.einsum("srd,dh->srh", block_rows, matrix, preferred_element_type=jnp.float32)
            for matrix in (w_query, key_weight, value_weight)
        ],
        axis=2,
    )
    token_positions = cache_lengths[:, None] + jnp.arange(new_rows, dtype=jnp.int32)[None, :]
    queries = apply_rotary(
        mixed_rows[..., :query_width].reshape(slots, new_rows, query_heads, HEAD_DIM),
        token_positions,
    ).astype(jnp.bfloat16)
    incoming_keys = apply_rotary(
        mixed_rows[..., query_width : query_width + key_width].reshape(
            slots, new_rows, key_heads, HEAD_DIM
        ),
        token_positions,
    ).astype(jnp.bfloat16)
    incoming_values = (
        mixed_rows[..., query_width + key_width :]
        .astype(jnp.bfloat16)
        .reshape(slots, new_rows, key_heads, HEAD_DIM)
    )
    new_keys = jnp.where(
        window_mask, incoming_keys.reshape(slots, new_rows, key_width), empty_value_rows
    )
    new_values = jnp.where(
        window_mask, incoming_values.reshape(slots, new_rows, key_width), empty_value_rows
    )
    padded = []
    for current_head_index in range(key_heads):
        head_queries = queries[
            :, :, current_head_index * query_group_count : (current_head_index + 1) * query_group_count, :
        ].reshape(slots, new_rows * query_group_count, HEAD_DIM)
        padded.append(
            jnp.pad(
                head_queries,
                ((0, 0), (0, 0), (current_head_index * HEAD_DIM, (key_heads - 1 - current_head_index) * HEAD_DIM)),
            )
        )
    attended_rows = attend_all(
        jnp.concatenate(padded, axis=1),
        cache_keys,
        stored_cache_values,
        incoming_keys.reshape(slots, new_rows, key_width),
        incoming_values.reshape(slots, new_rows, key_width),
        cache_lengths,
        query_group_count,
    )
    head_rows = new_rows * query_group_count
    attended = jnp.concatenate(
        [
            attended_rows[
                :, h * head_rows : (h + 1) * head_rows, h * HEAD_DIM : (h + 1) * HEAD_DIM
            ].reshape(slots, new_rows, query_group_count * HEAD_DIM)
            for h in range(key_heads)
        ],
        axis=2,
    )
    block_rows = attended
    projected = tok_reduce(
        jnp.einsum("sth,hd->std", block_rows, w_out, preferred_element_type=jnp.float32), 1
    )
    residual = (hidden_in.astype(jnp.float32) + projected).astype(jnp.bfloat16)
    spread_rows = lax.all_to_all(residual, "req", split_axis=1, concat_axis=0, tiled=True)
    picked_index = jnp.nonzero(live_slots > 0, size=lax.axis_size("req"), fill_value=0)[0].astype(
        jnp.int32
    )
    picked = jnp.take(spread_rows, picked_index, axis=0)
    completed_output = feed_forward(
        picked.reshape(-1, model_width), mlp_gain, w_gate, w_up, w_down
    ).reshape(picked.shape)
    placed = jnp.zeros_like(spread_rows).at[picked_index].set(completed_output)
    hidden_out = lax.all_to_all(placed, "req", split_axis=0, concat_axis=1, tiled=True)
    return (hidden_out, new_keys, new_values)


def solution(mesh):
    return jax.shard_map(
        local,
        mesh=mesh,
        in_specs=(
            P("req", "tok", None),
            P("req", None, "tok"),
            P("req", None, "tok"),
            P("req"),
            P(),
            P(),
            P(None, "tok"),
            P(None, "tok"),
            P(None, "tok"),
            P("tok", None),
            P(),
            P(None, "tok"),
            P(None, "tok"),
            P("tok", None),
        ),
        out_specs=(P("req", "tok", None), P("req", None, "tok"), P("req", None, "tok")),
        check_vma=False,
    )
```

```python
import functools

import jax
import jax.numpy as jnp
from jax import lax
from jax.experimental import pallas as pl
from jax.experimental.pallas import tpu as pltpu
from jax.sharding import PartitionSpec as P

HEAD_DIM = 80


EPSILON = 1e-05
ROPE_BASE = 10000.0


def rms_norm(values, norm_gain):
    widened = values.astype(jnp.float32)
    mean_square = jnp.mean(widened * widened, axis=-1, keepdims=True)
    return widened * lax.rsqrt(mean_square + EPSILON) * norm_gain


def tok_gather(part, axis):
    me = lax.axis_index("tok")
    other = lax.ppermute(part, "tok", [(0, 1), (1, 0)])
    first = jnp.where(me == 0, part, other)
    second = jnp.where(me == 0, other, part)
    return jnp.concatenate([first, second], axis=axis)


def tok_reduce(whole, axis):
    me = lax.axis_index("tok")
    half = whole.shape[axis] // 2
    low = lax.slice_in_dim(whole, 0, half, axis=axis)
    high = lax.slice_in_dim(whole, half, 2 * half, axis=axis)
    keep = jnp.where(me == 0, low, high)
    send = jnp.where(me == 0, high, low).astype(jnp.bfloat16)
    other = lax.ppermute(send, "tok", [(0, 1), (1, 0)])
    return keep + other.astype(jnp.float32)


def apply_rotary(values, token_positions):
    full_width = values.shape[-1]
    half_width = full_width // 2
    inverse = ROPE_BASE ** (-(jnp.arange(half_width, dtype=jnp.float32) * 2.0) / full_width)
    angles = token_positions.astype(jnp.float32)[..., None] * inverse
    cosine = jnp.cos(angles)[..., None, :]
    sine_part = jnp.sin(angles)[..., None, :]
    first_half = values[..., :half_width]
    second_half = values[..., half_width:]
    return jnp.concatenate(
        [
            first_half * cosine - second_half * sine_part,
            second_half * cosine + first_half * sine_part,
        ],
        axis=-1,
    )


NEG = -jnp.inf
KEY_BLOCK = 512


def attention_kernel(len_ref, q_ref, kc_ref, vc_ref, kn_ref, vn_ref, o_ref, *, group, scaling):
    slot = pl.program_id(0)
    rows = q_ref.shape[1]
    window = kc_ref.shape[1]
    fresh = kn_ref.shape[1]
    heads_rows = fresh * group
    length = len_ref[slot]
    q = q_ref[0]
    row = pl.program_id(1) * rows + lax.broadcasted_iota(jnp.int32, (rows, 1), 0)
    token = (row % heads_rows) // group
    dims = (((1,), (1,)), ((), ()))
    scores = lax.dot_general(q, kn_ref[0], dims, preferred_element_type=jnp.float32) * scaling
    fresh_pos = lax.broadcasted_iota(jnp.int32, (1, fresh), 1)
    scores = jnp.where(fresh_pos <= token, scores, NEG)
    top = jnp.max(scores, axis=1, keepdims=True)
    raised = jnp.exp(scores - top)
    mass = jnp.sum(raised, axis=1, keepdims=True)
    total = jnp.dot(raised.astype(jnp.bfloat16), vn_ref[0], preferred_element_type=jnp.float32)
    lowest = window - length
    first_block = jnp.maximum(lowest, 0) // KEY_BLOCK

    def body(block, carry):
        top, mass, total = carry
        begin = pl.multiple_of(block * KEY_BLOCK, KEY_BLOCK)
        keys = kc_ref[0, pl.ds(begin, KEY_BLOCK), :]
        values = vc_ref[0, pl.ds(begin, KEY_BLOCK), :]
        scores = lax.dot_general(q, keys, dims, preferred_element_type=jnp.float32) * scaling
        key_pos = begin + lax.broadcasted_iota(jnp.int32, (1, KEY_BLOCK), 1)
        visible = (key_pos >= lowest) & (key_pos > token)
        scores = jnp.where(visible, scores, NEG)
        raised_top = jnp.maximum(top, jnp.max(scores, axis=1, keepdims=True))
        shrink = jnp.exp(top - raised_top)
        raised = jnp.exp(scores - raised_top)
        mass = mass * shrink + jnp.sum(raised, axis=1, keepdims=True)
        total = total * shrink + jnp.dot(
            raised.astype(jnp.bfloat16), values, preferred_element_type=jnp.float32
        )
        return raised_top, mass, total

    top, mass, total = lax.fori_loop(first_block, window // KEY_BLOCK, body, (top, mass, total))
    o_ref[0] = (total / mass).astype(o_ref.dtype)


def attend_all(padded_queries, cache_keys, cache_values, fresh_keys, fresh_values, lengths, group):
    slots, total_rows, width = padded_queries.shape
    window = cache_keys.shape[1]
    fresh = fresh_keys.shape[1]
    rows = 512
    scaling = HEAD_DIM ** (-0.5)
    kernel = functools.partial(attention_kernel, group=group, scaling=scaling)
    flops = 2 * 2 * slots * total_rows * (window + fresh) * width
    cost = pl.CostEstimate(
        flops=flops,
        transcendentals=slots * total_rows * (window + fresh),
        bytes_accessed=2 * (2 * padded_queries.size + 2 * cache_keys.size + 2 * fresh_keys.size),
    )
    return pl.pallas_call(
        kernel,
        grid_spec=pltpu.PrefetchScalarGridSpec(
            num_scalar_prefetch=1,
            grid=(slots, total_rows // rows),
            in_specs=[
                pl.BlockSpec((1, rows, width), lambda s, r, n: (s, r, 0)),
                pl.BlockSpec((1, window, width), lambda s, r, n: (s, 0, 0)),
                pl.BlockSpec((1, window, width), lambda s, r, n: (s, 0, 0)),
                pl.BlockSpec((1, fresh, width), lambda s, r, n: (s, 0, 0)),
                pl.BlockSpec((1, fresh, width), lambda s, r, n: (s, 0, 0)),
            ],
            out_specs=pl.BlockSpec((1, rows, width), lambda s, r, n: (s, r, 0)),
        ),
        out_shape=jax.ShapeDtypeStruct((slots, total_rows, width), jnp.bfloat16),
        compiler_params=pltpu.CompilerParams(dimension_semantics=("arbitrary", "arbitrary")),
        cost_estimate=cost,
    )(lengths, padded_queries, cache_keys, cache_values, fresh_keys, fresh_values)


def feed_forward(rows_in, mlp_gain, w_gate, w_up, w_down):
    normed_rows = rms_norm(rows_in, mlp_gain).astype(jnp.bfloat16)
    block_rows = tok_gather(normed_rows, 0)
    gate_part = jnp.dot(block_rows, w_gate, preferred_element_type=jnp.float32)
    up_part = jnp.dot(block_rows, w_up, preferred_element_type=jnp.float32)
    activated = (jax.nn.silu(gate_part) * up_part).astype(jnp.bfloat16)
    summed = tok_reduce(
        jnp.dot(activated, w_down, preferred_element_type=jnp.float32), 0
    )
    return (rows_in.astype(jnp.float32) + summed).astype(jnp.bfloat16)


def local(
    hidden_in,
    cache_keys,
    stored_cache_values,
    cache_lengths,
    live_slots,
    attn_gain,
    w_query,
    key_weight,
    value_weight,
    w_out,
    mlp_gain,
    w_gate,
    w_up,
    w_down,
):
    slots, quarter, model_width = hidden_in.shape
    new_rows = quarter * lax.axis_size("tok")
    query_width = w_query.shape[1]
    key_width = key_weight.shape[1]
    query_heads = query_width // HEAD_DIM
    key_heads = key_width // HEAD_DIM
    query_group_count = query_heads // key_heads
    alive_slots = lax.dynamic_slice_in_dim(live_slots, lax.axis_index("req") * slots, slots)
    window_mask = alive_slots[:, None, None] > 0
    empty_value_rows = jnp.zeros((), jnp.bfloat16)
    normed = rms_norm(hidden_in, attn_gain).astype(jnp.bfloat16)
    block_rows = tok_gather(normed, 1)
    mixed_rows = jnp.concatenate(
        [
            jnp.einsum("srd,dh->srh", block_rows, matrix, preferred_element_type=jnp.float32)
            for matrix in (w_query, key_weight, value_weight)
        ],
        axis=2,
    )
    token_positions = cache_lengths[:, None] + jnp.arange(new_rows, dtype=jnp.int32)[None, :]
    queries = apply_rotary(
        mixed_rows[..., :query_width].reshape(slots, new_rows, query_heads, HEAD_DIM),
        token_positions,
    ).astype(jnp.bfloat16)
    incoming_keys = apply_rotary(
        mixed_rows[..., query_width : query_width + key_width].reshape(
            slots, new_rows, key_heads, HEAD_DIM
        ),
        token_positions,
    ).astype(jnp.bfloat16)
    incoming_values = (
        mixed_rows[..., query_width + key_width :]
        .astype(jnp.bfloat16)
        .reshape(slots, new_rows, key_heads, HEAD_DIM)
    )
    new_keys = jnp.where(
        window_mask, incoming_keys.reshape(slots, new_rows, key_width), empty_value_rows
    )
    new_values = jnp.where(
        window_mask, incoming_values.reshape(slots, new_rows, key_width), empty_value_rows
    )
    padded = []
    for current_head_index in range(key_heads):
        head_queries = queries[
            :, :, current_head_index * query_group_count : (current_head_index + 1) * query_group_count, :
        ].reshape(slots, new_rows * query_group_count, HEAD_DIM)
        padded.append(
            jnp.pad(
                head_queries,
                ((0, 0), (0, 0), (current_head_index * HEAD_DIM, (key_heads - 1 - current_head_index) * HEAD_DIM)),
            )
        )
    attended_rows = attend_all(
        jnp.concatenate(padded, axis=1),
        cache_keys,
        stored_cache_values,
        incoming_keys.reshape(slots, new_rows, key_width),
        incoming_values.reshape(slots, new_rows, key_width),
        cache_lengths,
        query_group_count,
    )
    head_rows = new_rows * query_group_count
    attended = jnp.concatenate(
        [
            attended_rows[
                :, h * head_rows : (h + 1) * head_rows, h * HEAD_DIM : (h + 1) * HEAD_DIM
            ].reshape(slots, new_rows, query_group_count * HEAD_DIM)
            for h in range(key_heads)
        ],
        axis=2,
    )
    block_rows = attended
    projected = tok_reduce(
        jnp.einsum("sth,hd->std", block_rows, w_out, preferred_element_type=jnp.float32), 1
    )
    residual = (hidden_in.astype(jnp.float32) + projected).astype(jnp.bfloat16)
    rows = residual.reshape(-1, model_width)
    mlp_in = rms_norm(rows, mlp_gain).astype(jnp.bfloat16)
    partner_in = lax.ppermute(mlp_in, "tok", [(0, 1), (1, 0)])

    def hidden_half(block):
        gate_part = jnp.dot(block, w_gate, preferred_element_type=jnp.float32)
        up_part = jnp.dot(block, w_up, preferred_element_type=jnp.float32)
        activated = (jax.nn.silu(gate_part) * up_part).astype(jnp.bfloat16)
        return jnp.dot(activated, w_down, preferred_element_type=jnp.float32)

    own_part = hidden_half(mlp_in)
    partner_part = lax.ppermute(
        hidden_half(partner_in).astype(jnp.bfloat16), "tok", [(0, 1), (1, 0)]
    )
    completed = (
        rows.astype(jnp.float32) + (own_part + partner_part.astype(jnp.float32))
    ).astype(jnp.bfloat16)
    hidden_out = jnp.where(
        window_mask, completed.reshape(hidden_in.shape), empty_value_rows
    )
    return (hidden_out, new_keys, new_values)


def solution(mesh):
    return jax.shard_map(
        local,
        mesh=mesh,
        in_specs=(
            P("req", "tok", None),
            P("req", None, "tok"),
            P("req", None, "tok"),
            P("req"),
            P(),
            P(),
            P(None, "tok"),
            P(None, "tok"),
            P(None, "tok"),
            P("tok", None),
            P(),
            P(None, "tok"),
            P(None, "tok"),
            P("tok", None),
        ),
        out_specs=(P("req", "tok", None), P("req", None, "tok"), P("req", None, "tok")),
        check_vma=False,
    )
```

```python
import functools

import jax
import jax.numpy as jnp
from jax import lax
from jax.experimental import pallas as pl
from jax.experimental.pallas import tpu as pltpu
from jax.sharding import PartitionSpec as P

HEAD_DIM = 80


EPSILON = 1e-05
ROPE_BASE = 10000.0


def rms_norm(values, norm_gain):
    widened = values.astype(jnp.float32)
    mean_square = jnp.mean(widened * widened, axis=-1, keepdims=True)
    return widened * lax.rsqrt(mean_square + EPSILON) * norm_gain


def tok_gather(part, axis):
    me = lax.axis_index("tok")
    other = lax.ppermute(part, "tok", [(0, 1), (1, 0)])
    first = jnp.where(me == 0, part, other)
    second = jnp.where(me == 0, other, part)
    return jnp.concatenate([first, second], axis=axis)


def tok_reduce(whole, axis):
    me = lax.axis_index("tok")
    half = whole.shape[axis] // 2
    low = lax.slice_in_dim(whole, 0, half, axis=axis)
    high = lax.slice_in_dim(whole, half, 2 * half, axis=axis)
    keep = jnp.where(me == 0, low, high)
    send = jnp.where(me == 0, high, low).astype(jnp.bfloat16)
    other = lax.ppermute(send, "tok", [(0, 1), (1, 0)])
    return keep + other.astype(jnp.float32)


def apply_rotary(values, token_positions):
    full_width = values.shape[-1]
    half_width = full_width // 2
    inverse = ROPE_BASE ** (-(jnp.arange(half_width, dtype=jnp.float32) * 2.0) / full_width)
    angles = token_positions.astype(jnp.float32)[..., None] * inverse
    cosine = jnp.cos(angles)[..., None, :]
    sine_part = jnp.sin(angles)[..., None, :]
    first_half = values[..., :half_width]
    second_half = values[..., half_width:]
    return jnp.concatenate(
        [
            first_half * cosine - second_half * sine_part,
            second_half * cosine + first_half * sine_part,
        ],
        axis=-1,
    )


NEG = -jnp.inf
KEY_BLOCK = 512


def attention_kernel(len_ref, q_ref, kc_ref, vc_ref, kn_ref, vn_ref, o_ref, *, group, scaling):
    slot = pl.program_id(0)
    rows = q_ref.shape[1]
    window = kc_ref.shape[2]
    fresh = kn_ref.shape[1]
    heads_rows = fresh * group
    blocks = window // KEY_BLOCK
    length = len_ref[slot]
    q = q_ref[0]
    row = pl.program_id(1) * rows + lax.broadcasted_iota(jnp.int32, (rows, 1), 0)
    token = (row % heads_rows) // group
    transposed = (((1,), (1,)), ((), ()))
    scores = lax.dot_general(q, kn_ref[0], transposed, preferred_element_type=jnp.float32) * scaling
    fresh_pos = lax.broadcasted_iota(jnp.int32, (1, fresh), 1)
    scores = jnp.where(fresh_pos <= token, scores, NEG)
    top = jnp.max(scores, axis=1, keepdims=True)
    raised = jnp.exp(scores - top)
    mass = jnp.sum(raised, axis=1, keepdims=True)
    total = jnp.dot(raised.astype(jnp.bfloat16), vn_ref[0], preferred_element_type=jnp.float32)
    lowest = window - length
    first_block = jnp.minimum(jnp.maximum(lowest, 0) // KEY_BLOCK, blocks - 1)

    def step(block, carry, masked):
        top, mass, total = carry
        begin = pl.multiple_of(block * KEY_BLOCK, KEY_BLOCK)
        keys = kc_ref[0, :, pl.ds(begin, KEY_BLOCK)]
        values = vc_ref[0, :, pl.ds(begin, KEY_BLOCK)]
        scores = jnp.dot(q, keys, preferred_element_type=jnp.float32) * scaling
        if masked:
            key_pos = begin + lax.broadcasted_iota(jnp.int32, (1, KEY_BLOCK), 1)
            visible = (key_pos >= lowest) & (key_pos > token)
            scores = jnp.where(visible, scores, NEG)
        raised_top = jnp.maximum(top, jnp.max(scores, axis=1, keepdims=True))
        shrink = jnp.exp(top - raised_top)
        raised = jnp.exp(scores - raised_top)
        mass = mass * shrink + jnp.sum(raised, axis=1, keepdims=True)
        total = total * shrink + lax.dot_general(
            raised.astype(jnp.bfloat16), values, transposed, preferred_element_type=jnp.float32
        )
        return raised_top, mass, total

    carry = step(first_block, (top, mass, total), True)
    top, mass, total = lax.fori_loop(
        first_block + 1, blocks, lambda b, c: step(b, c, False), carry
    )
    o_ref[0] = (total / mass).astype(o_ref.dtype)


def attend_all(padded_queries, cache_keys, cache_values, fresh_keys, fresh_values, lengths, group):
    slots, total_rows, width = padded_queries.shape
    window = cache_keys.shape[2]
    fresh = fresh_keys.shape[1]
    rows = 512
    scaling = HEAD_DIM ** (-0.5)
    kernel = functools.partial(attention_kernel, group=group, scaling=scaling)
    flops = 2 * 2 * slots * total_rows * (window + fresh) * width
    cost = pl.CostEstimate(
        flops=flops,
        transcendentals=slots * total_rows * (window + fresh),
        bytes_accessed=2 * (2 * padded_queries.size + 2 * cache_keys.size + 2 * fresh_keys.size),
    )
    return pl.pallas_call(
        kernel,
        grid_spec=pltpu.PrefetchScalarGridSpec(
            num_scalar_prefetch=1,
            grid=(slots, total_rows // rows),
            in_specs=[
                pl.BlockSpec((1, rows, width), lambda s, r, n: (s, r, 0)),
                pl.BlockSpec((1, width, window), lambda s, r, n: (s, 0, 0)),
                pl.BlockSpec((1, width, window), lambda s, r, n: (s, 0, 0)),
                pl.BlockSpec((1, fresh, width), lambda s, r, n: (s, 0, 0)),
                pl.BlockSpec((1, fresh, width), lambda s, r, n: (s, 0, 0)),
            ],
            out_specs=pl.BlockSpec((1, rows, width), lambda s, r, n: (s, r, 0)),
        ),
        out_shape=jax.ShapeDtypeStruct((slots, total_rows, width), jnp.bfloat16),
        compiler_params=pltpu.CompilerParams(dimension_semantics=("arbitrary", "arbitrary")),
        cost_estimate=cost,
    )(lengths, padded_queries, cache_keys, cache_values, fresh_keys, fresh_values)


def feed_forward(rows_in, mlp_gain, w_gate, w_up, w_down):
    normed_rows = rms_norm(rows_in, mlp_gain).astype(jnp.bfloat16)
    block_rows = tok_gather(normed_rows, 0)
    gate_part = jnp.dot(block_rows, w_gate, preferred_element_type=jnp.float32)
    up_part = jnp.dot(block_rows, w_up, preferred_element_type=jnp.float32)
    activated = (jax.nn.silu(gate_part) * up_part).astype(jnp.bfloat16)
    summed = tok_reduce(
        jnp.dot(activated, w_down, preferred_element_type=jnp.float32), 0
    )
    return (rows_in.astype(jnp.float32) + summed).astype(jnp.bfloat16)


def local(
    hidden_in,
    cache_keys,
    stored_cache_values,
    cache_lengths,
    live_slots,
    attn_gain,
    w_query,
    key_weight,
    value_weight,
    w_out,
    mlp_gain,
    w_gate,
    w_up,
    w_down,
):
    slots, quarter, model_width = hidden_in.shape
    new_rows = quarter * lax.axis_size("tok")
    query_width = w_query.shape[1]
    key_width = key_weight.shape[1]
    query_heads = query_width // HEAD_DIM
    key_heads = key_width // HEAD_DIM
    query_group_count = query_heads // key_heads
    alive_slots = lax.dynamic_slice_in_dim(live_slots, lax.axis_index("req") * slots, slots)
    window_mask = alive_slots[:, None, None] > 0
    empty_value_rows = jnp.zeros((), jnp.bfloat16)
    normed = rms_norm(hidden_in, attn_gain).astype(jnp.bfloat16)
    block_rows = tok_gather(normed, 1)
    mixed_rows = jnp.concatenate(
        [
            jnp.einsum("srd,dh->srh", block_rows, matrix, preferred_element_type=jnp.float32)
            for matrix in (w_query, key_weight, value_weight)
        ],
        axis=2,
    )
    token_positions = cache_lengths[:, None] + jnp.arange(new_rows, dtype=jnp.int32)[None, :]
    queries = apply_rotary(
        mixed_rows[..., :query_width].reshape(slots, new_rows, query_heads, HEAD_DIM),
        token_positions,
    ).astype(jnp.bfloat16)
    incoming_keys = apply_rotary(
        mixed_rows[..., query_width : query_width + key_width].reshape(
            slots, new_rows, key_heads, HEAD_DIM
        ),
        token_positions,
    ).astype(jnp.bfloat16)
    incoming_values = (
        mixed_rows[..., query_width + key_width :]
        .astype(jnp.bfloat16)
        .reshape(slots, new_rows, key_heads, HEAD_DIM)
    )
    new_keys = jnp.where(
        window_mask, incoming_keys.reshape(slots, new_rows, key_width), empty_value_rows
    )
    new_values = jnp.where(
        window_mask, incoming_values.reshape(slots, new_rows, key_width), empty_value_rows
    )
    padded = []
    for current_head_index in range(key_heads):
        head_queries = queries[
            :, :, current_head_index * query_group_count : (current_head_index + 1) * query_group_count, :
        ].reshape(slots, new_rows * query_group_count, HEAD_DIM)
        padded.append(
            jnp.pad(
                head_queries,
                ((0, 0), (0, 0), (current_head_index * HEAD_DIM, (key_heads - 1 - current_head_index) * HEAD_DIM)),
            )
        )
    attended_rows = attend_all(
        jnp.concatenate(padded, axis=1),
        jnp.swapaxes(cache_keys, 1, 2),
        jnp.swapaxes(stored_cache_values, 1, 2),
        incoming_keys.reshape(slots, new_rows, key_width),
        incoming_values.reshape(slots, new_rows, key_width),
        cache_lengths,
        query_group_count,
    )
    head_rows = new_rows * query_group_count
    attended = jnp.concatenate(
        [
            attended_rows[
                :, h * head_rows : (h + 1) * head_rows, h * HEAD_DIM : (h + 1) * HEAD_DIM
            ].reshape(slots, new_rows, query_group_count * HEAD_DIM)
            for h in range(key_heads)
        ],
        axis=2,
    )
    block_rows = attended
    projected = tok_reduce(
        jnp.einsum("sth,hd->std", block_rows, w_out, preferred_element_type=jnp.float32), 1
    )
    residual = (hidden_in.astype(jnp.float32) + projected).astype(jnp.bfloat16)
    rows = residual.reshape(-1, model_width)
    mlp_in = rms_norm(rows, mlp_gain).astype(jnp.bfloat16)
    partner_in = lax.ppermute(mlp_in, "tok", [(0, 1), (1, 0)])

    def hidden_half(block):
        gate_part = jnp.dot(block, w_gate, preferred_element_type=jnp.float32)
        up_part = jnp.dot(block, w_up, preferred_element_type=jnp.float32)
        activated = (jax.nn.silu(gate_part) * up_part).astype(jnp.bfloat16)
        return jnp.dot(activated, w_down, preferred_element_type=jnp.float32)

    own_part = hidden_half(mlp_in)
    partner_part = lax.ppermute(
        hidden_half(partner_in).astype(jnp.bfloat16), "tok", [(0, 1), (1, 0)]
    )
    completed = (
        rows.astype(jnp.float32) + (own_part + partner_part.astype(jnp.float32))
    ).astype(jnp.bfloat16)
    hidden_out = jnp.where(
        window_mask, completed.reshape(hidden_in.shape), empty_value_rows
    )
    return (hidden_out, new_keys, new_values)


def solution(mesh):
    return jax.shard_map(
        local,
        mesh=mesh,
        in_specs=(
            P("req", "tok", None),
            P("req", None, "tok"),
            P("req", None, "tok"),
            P("req"),
            P(),
            P(),
            P(None, "tok"),
            P(None, "tok"),
            P(None, "tok"),
            P("tok", None),
            P(),
            P(None, "tok"),
            P(None, "tok"),
            P("tok", None),
        ),
        out_specs=(P("req", "tok", None), P("req", None, "tok"), P("req", None, "tok")),
        check_vma=False,
    )
```

```python
import functools

import jax
import jax.numpy as jnp
from jax import lax
from jax.experimental import pallas as pl
from jax.experimental.pallas import tpu as pltpu
from jax.sharding import PartitionSpec as P

HEAD_DIM = 80


EPSILON = 1e-05
ROPE_BASE = 10000.0


def rms_norm(values, norm_gain):
    widened = values.astype(jnp.float32)
    mean_square = jnp.mean(widened * widened, axis=-1, keepdims=True)
    return widened * lax.rsqrt(mean_square + EPSILON) * norm_gain


def tok_gather(part, axis):
    me = lax.axis_index("tok")
    other = lax.ppermute(part, "tok", [(0, 1), (1, 0)])
    first = jnp.where(me == 0, part, other)
    second = jnp.where(me == 0, other, part)
    return jnp.concatenate([first, second], axis=axis)


def tok_reduce(whole, axis):
    me = lax.axis_index("tok")
    half = whole.shape[axis] // 2
    low = lax.slice_in_dim(whole, 0, half, axis=axis)
    high = lax.slice_in_dim(whole, half, 2 * half, axis=axis)
    keep = jnp.where(me == 0, low, high)
    send = jnp.where(me == 0, high, low).astype(jnp.bfloat16)
    other = lax.ppermute(send, "tok", [(0, 1), (1, 0)])
    return keep + other.astype(jnp.float32)


def apply_rotary(values, token_positions):
    full_width = values.shape[-1]
    half_width = full_width // 2
    inverse = ROPE_BASE ** (-(jnp.arange(half_width, dtype=jnp.float32) * 2.0) / full_width)
    angles = token_positions.astype(jnp.float32)[..., None] * inverse
    cosine = jnp.cos(angles)[..., None, :]
    sine_part = jnp.sin(angles)[..., None, :]
    first_half = values[..., :half_width]
    second_half = values[..., half_width:]
    return jnp.concatenate(
        [
            first_half * cosine - second_half * sine_part,
            second_half * cosine + first_half * sine_part,
        ],
        axis=-1,
    )


NEG = -jnp.inf
KEY_BLOCK = 512


def attention_kernel(len_ref, q_ref, kc_ref, vc_ref, kn_ref, vn_ref, o_ref, *, group, scaling):
    slot = pl.program_id(0)
    rows = q_ref.shape[1]
    window = kc_ref.shape[2]
    fresh = kn_ref.shape[1]
    heads_rows = fresh * group
    blocks = window // KEY_BLOCK
    length = len_ref[slot]
    q = q_ref[0]
    row = pl.program_id(1) * rows + lax.broadcasted_iota(jnp.int32, (rows, 1), 0)
    token = (row % heads_rows) // group
    transposed = (((1,), (1,)), ((), ()))
    scores = lax.dot_general(q, kn_ref[0], transposed, preferred_element_type=jnp.float32) * scaling
    fresh_pos = lax.broadcasted_iota(jnp.int32, (1, fresh), 1)
    scores = jnp.where(fresh_pos <= token, scores, NEG)
    top = jnp.max(scores, axis=1, keepdims=True)
    raised = jnp.exp(scores - top)
    mass = jnp.sum(raised, axis=1, keepdims=True)
    total = jnp.dot(raised.astype(jnp.bfloat16), vn_ref[0], preferred_element_type=jnp.float32)
    lowest = window - length
    first_block = jnp.minimum(jnp.maximum(lowest, 0) // KEY_BLOCK, blocks - 1)

    def step(block, carry, masked):
        top, mass, total = carry
        begin = pl.multiple_of(block * KEY_BLOCK, KEY_BLOCK)
        keys = kc_ref[0, :, pl.ds(begin, KEY_BLOCK)]
        values = vc_ref[0, :, pl.ds(begin, KEY_BLOCK)]
        scores = jnp.dot(q, keys, preferred_element_type=jnp.float32) * scaling
        if masked:
            key_pos = begin + lax.broadcasted_iota(jnp.int32, (1, KEY_BLOCK), 1)
            visible = (key_pos >= lowest) & (key_pos > token)
            scores = jnp.where(visible, scores, NEG)
        raised_top = jnp.maximum(top, jnp.max(scores, axis=1, keepdims=True))
        shrink = jnp.exp(top - raised_top)
        raised = jnp.exp(scores - raised_top)
        mass = mass * shrink + jnp.sum(raised, axis=1, keepdims=True)
        total = total * shrink + lax.dot_general(
            raised.astype(jnp.bfloat16), values, transposed, preferred_element_type=jnp.float32
        )
        return raised_top, mass, total

    carry = step(first_block, (top, mass, total), True)
    top, mass, total = lax.fori_loop(
        first_block + 1, blocks, lambda b, c: step(b, c, False), carry
    )
    o_ref[0] = (total / mass).astype(o_ref.dtype)


def attend_all(padded_queries, cache_keys, cache_values, fresh_keys, fresh_values, lengths, group):
    slots, total_rows, width = padded_queries.shape
    window = cache_keys.shape[2]
    fresh = fresh_keys.shape[1]
    rows = 512
    scaling = HEAD_DIM ** (-0.5)
    kernel = functools.partial(attention_kernel, group=group, scaling=scaling)
    flops = 2 * 2 * slots * total_rows * (window + fresh) * width
    cost = pl.CostEstimate(
        flops=flops,
        transcendentals=slots * total_rows * (window + fresh),
        bytes_accessed=2 * (2 * padded_queries.size + 2 * cache_keys.size + 2 * fresh_keys.size),
    )
    return pl.pallas_call(
        kernel,
        grid_spec=pltpu.PrefetchScalarGridSpec(
            num_scalar_prefetch=1,
            grid=(slots, total_rows // rows),
            in_specs=[
                pl.BlockSpec((1, rows, width), lambda s, r, n: (s, r, 0)),
                pl.BlockSpec((1, width, window), lambda s, r, n: (s, 0, 0)),
                pl.BlockSpec((1, width, window), lambda s, r, n: (s, 0, 0)),
                pl.BlockSpec((1, fresh, width), lambda s, r, n: (s, 0, 0)),
                pl.BlockSpec((1, fresh, width), lambda s, r, n: (s, 0, 0)),
            ],
            out_specs=pl.BlockSpec((1, rows, width), lambda s, r, n: (s, r, 0)),
        ),
        out_shape=jax.ShapeDtypeStruct((slots, total_rows, width), jnp.bfloat16),
        compiler_params=pltpu.CompilerParams(dimension_semantics=("arbitrary", "arbitrary")),
        cost_estimate=cost,
    )(lengths, padded_queries, cache_keys, cache_values, fresh_keys, fresh_values)


def feed_forward(rows_in, mlp_gain, w_gate, w_up, w_down):
    normed_rows = rms_norm(rows_in, mlp_gain).astype(jnp.bfloat16)
    block_rows = tok_gather(normed_rows, 0)
    gate_part = jnp.dot(block_rows, w_gate, preferred_element_type=jnp.float32)
    up_part = jnp.dot(block_rows, w_up, preferred_element_type=jnp.float32)
    activated = (jax.nn.silu(gate_part) * up_part).astype(jnp.bfloat16)
    summed = tok_reduce(
        jnp.dot(activated, w_down, preferred_element_type=jnp.float32), 0
    )
    return (rows_in.astype(jnp.float32) + summed).astype(jnp.bfloat16)


def swap_tok(part):
    return lax.ppermute(part, "tok", [(0, 1), (1, 0)])


def in_token_order(own, other):
    me = lax.axis_index("tok")
    first = jnp.where(me == 0, own, other)
    second = jnp.where(me == 0, other, own)
    return jnp.concatenate([first, second], axis=0)


def split_token_order(whole):
    me = lax.axis_index("tok")
    half = whole.shape[0] // 2
    low, high = whole[:half], whole[half:]
    return jnp.where(me == 0, low, high), jnp.where(me == 0, high, low)


def local(
    hidden_in,
    cache_keys,
    stored_cache_values,
    cache_lengths,
    live_slots,
    attn_gain,
    w_query,
    key_weight,
    value_weight,
    w_out,
    mlp_gain,
    w_gate,
    w_up,
    w_down,
):
    slots, quarter, model_width = hidden_in.shape
    new_rows = quarter * lax.axis_size("tok")
    query_width = w_query.shape[1]
    key_width = key_weight.shape[1]
    query_heads = query_width // HEAD_DIM
    key_heads = key_width // HEAD_DIM
    query_group_count = query_heads // key_heads
    head_rows = new_rows * query_group_count
    alive_slots = lax.dynamic_slice_in_dim(live_slots, lax.axis_index("req") * slots, slots)
    empty_value_rows = jnp.zeros((), jnp.bfloat16)
    keys_t = jnp.swapaxes(cache_keys, 1, 2)
    values_t = jnp.swapaxes(stored_cache_values, 1, 2)

    def hidden_half(block):
        gate_part = jnp.dot(block, w_gate, preferred_element_type=jnp.float32)
        up_part = jnp.dot(block, w_up, preferred_element_type=jnp.float32)
        activated = (jax.nn.silu(gate_part) * up_part).astype(jnp.bfloat16)
        return jnp.dot(activated, w_down, preferred_element_type=jnp.float32)

    outs, keys_out, values_out = [], [], []
    for slot in range(slots):
        alive = alive_slots[slot] > 0
        length = cache_lengths[slot]
        tokens = hidden_in[slot]
        normed = rms_norm(tokens, attn_gain).astype(jnp.bfloat16)
        block_rows = in_token_order(normed, swap_tok(normed))
        queries = jnp.dot(block_rows, w_query, preferred_element_type=jnp.float32)
        fresh_keys = jnp.dot(block_rows, key_weight, preferred_element_type=jnp.float32)
        fresh_values = jnp.dot(block_rows, value_weight, preferred_element_type=jnp.float32)
        token_positions = length + jnp.arange(new_rows, dtype=jnp.int32)
        queries = apply_rotary(
            queries.reshape(new_rows, query_heads, HEAD_DIM), token_positions
        ).astype(jnp.bfloat16)
        fresh_keys = apply_rotary(
            fresh_keys.reshape(new_rows, key_heads, HEAD_DIM), token_positions
        ).astype(jnp.bfloat16).reshape(new_rows, key_width)
        fresh_values = fresh_values.astype(jnp.bfloat16)
        keys_out.append(jnp.where(alive, fresh_keys, empty_value_rows))
        values_out.append(jnp.where(alive, fresh_values, empty_value_rows))
        padded = []
        for head in range(key_heads):
            head_queries = queries[
                :, head * query_group_count : (head + 1) * query_group_count, :
            ].reshape(head_rows, HEAD_DIM)
            padded.append(
                jnp.pad(
                    head_queries,
                    ((0, 0), (head * HEAD_DIM, (key_heads - 1 - head) * HEAD_DIM)),
                )
            )
        attended_rows = attend_all(
            jnp.concatenate(padded, axis=0)[None],
            keys_t[slot : slot + 1],
            values_t[slot : slot + 1],
            fresh_keys[None],
            fresh_values[None],
            cache_lengths[slot : slot + 1],
            query_group_count,
        )[0]
        attended = jnp.concatenate(
            [
                attended_rows[
                    h * head_rows : (h + 1) * head_rows, h * HEAD_DIM : (h + 1) * HEAD_DIM
                ].reshape(new_rows, query_group_count * HEAD_DIM)
                for h in range(key_heads)
            ],
            axis=1,
        )
        projected = jnp.dot(attended, w_out, preferred_element_type=jnp.float32)
        own_proj, other_proj = split_token_order(projected)
        received = swap_tok(other_proj.astype(jnp.bfloat16)).astype(jnp.float32)
        residual = (tokens.astype(jnp.float32) + (own_proj + received)).astype(jnp.bfloat16)
        mlp_in = rms_norm(residual, mlp_gain).astype(jnp.bfloat16)
        both = hidden_half(jnp.concatenate([mlp_in, swap_tok(mlp_in)], axis=0))
        own_part = both[:quarter]
        partner_part = swap_tok(both[quarter:].astype(jnp.bfloat16)).astype(jnp.float32)
        completed = (
            residual.astype(jnp.float32) + (own_part + partner_part)
        ).astype(jnp.bfloat16)
        outs.append(jnp.where(alive, completed, empty_value_rows))
    return (jnp.stack(outs), jnp.stack(keys_out), jnp.stack(values_out))


def solution(mesh):
    return jax.shard_map(
        local,
        mesh=mesh,
        in_specs=(
            P("req", "tok", None),
            P("req", None, "tok"),
            P("req", None, "tok"),
            P("req"),
            P(),
            P(),
            P(None, "tok"),
            P(None, "tok"),
            P(None, "tok"),
            P("tok", None),
            P(),
            P(None, "tok"),
            P(None, "tok"),
            P("tok", None),
        ),
        out_specs=(P("req", "tok", None), P("req", None, "tok"), P("req", None, "tok")),
        check_vma=False,
    )
```

```python
import functools

import jax
import jax.numpy as jnp
from jax import lax
from jax.experimental import pallas as pl
from jax.experimental.pallas import tpu as pltpu
from jax.sharding import PartitionSpec as P

HEAD_DIM = 80


EPSILON = 1e-05
ROPE_BASE = 10000.0


def rms_norm(values, norm_gain):
    widened = values.astype(jnp.float32)
    mean_square = jnp.mean(widened * widened, axis=-1, keepdims=True)
    return widened * lax.rsqrt(mean_square + EPSILON) * norm_gain


def tok_gather(part, axis):
    me = lax.axis_index("tok")
    other = lax.ppermute(part, "tok", [(0, 1), (1, 0)])
    first = jnp.where(me == 0, part, other)
    second = jnp.where(me == 0, other, part)
    return jnp.concatenate([first, second], axis=axis)


def tok_reduce(whole, axis):
    me = lax.axis_index("tok")
    half = whole.shape[axis] // 2
    low = lax.slice_in_dim(whole, 0, half, axis=axis)
    high = lax.slice_in_dim(whole, half, 2 * half, axis=axis)
    keep = jnp.where(me == 0, low, high)
    send = jnp.where(me == 0, high, low).astype(jnp.bfloat16)
    other = lax.ppermute(send, "tok", [(0, 1), (1, 0)])
    return keep + other.astype(jnp.float32)


def apply_rotary(values, token_positions):
    full_width = values.shape[-1]
    half_width = full_width // 2
    inverse = ROPE_BASE ** (-(jnp.arange(half_width, dtype=jnp.float32) * 2.0) / full_width)
    angles = token_positions.astype(jnp.float32)[..., None] * inverse
    cosine = jnp.cos(angles)[..., None, :]
    sine_part = jnp.sin(angles)[..., None, :]
    first_half = values[..., :half_width]
    second_half = values[..., half_width:]
    return jnp.concatenate(
        [
            first_half * cosine - second_half * sine_part,
            second_half * cosine + first_half * sine_part,
        ],
        axis=-1,
    )


NEG = -jnp.inf
KEY_BLOCK = 1024
LOG2E = 1.4426950408889634


def attention_kernel(len_ref, q_ref, kc_ref, vc_ref, kn_ref, vn_ref, o_ref, *, group, scaling):
    slot = pl.program_id(0)
    rows = q_ref.shape[1]
    window = kc_ref.shape[2]
    fresh = kn_ref.shape[1]
    heads_rows = fresh * group
    blocks = window // KEY_BLOCK
    length = len_ref[slot]
    q = q_ref[0]
    row = pl.program_id(1) * rows + lax.broadcasted_iota(jnp.int32, (rows, 1), 0)
    token = (row % heads_rows) // group
    transposed = (((1,), (1,)), ((), ()))
    scores = lax.dot_general(q, kn_ref[0], transposed, preferred_element_type=jnp.float32) * scaling
    fresh_pos = lax.broadcasted_iota(jnp.int32, (1, fresh), 1)
    scores = jnp.where(fresh_pos <= token, scores, NEG)
    top = jnp.max(scores, axis=1, keepdims=True)
    raised = jnp.exp2(scores - top)
    mass = jnp.sum(raised, axis=1, keepdims=True)
    total = jnp.dot(raised.astype(jnp.bfloat16), vn_ref[0], preferred_element_type=jnp.float32)
    lowest = window - length
    first_block = jnp.minimum(jnp.maximum(lowest, 0) // KEY_BLOCK, blocks - 1)

    def step(block, carry, masked):
        top, mass, total = carry
        begin = pl.multiple_of(block * KEY_BLOCK, KEY_BLOCK)
        keys = kc_ref[0, :, pl.ds(begin, KEY_BLOCK)]
        values = vc_ref[0, :, pl.ds(begin, KEY_BLOCK)]
        scores = jnp.dot(q, keys, preferred_element_type=jnp.float32) * scaling
        if masked:
            key_pos = begin + lax.broadcasted_iota(jnp.int32, (1, KEY_BLOCK), 1)
            visible = (key_pos >= lowest) & (key_pos > token)
            scores = jnp.where(visible, scores, NEG)
        raised_top = jnp.maximum(top, jnp.max(scores, axis=1, keepdims=True))
        shrink = jnp.exp2(top - raised_top)
        raised = jnp.exp2(scores - raised_top)
        mass = mass * shrink + jnp.sum(raised, axis=1, keepdims=True)
        total = total * shrink + lax.dot_general(
            raised.astype(jnp.bfloat16),
            values,
            transposed,
            preferred_element_type=jnp.float32,
        )
        return raised_top, mass, total

    carry = step(first_block, (top, mass, total), True)
    top, mass, total = lax.fori_loop(
        first_block + 1, blocks, lambda b, c: step(b, c, False), carry
    )
    o_ref[0] = (total / mass).astype(o_ref.dtype)


def attend_all(padded_queries, cache_keys, cache_values, fresh_keys, fresh_values, lengths, group, rows=2048):
    slots, total_rows, width = padded_queries.shape
    window = cache_keys.shape[2]
    fresh = fresh_keys.shape[1]

    scaling = HEAD_DIM ** (-0.5) * LOG2E
    kernel = functools.partial(attention_kernel, group=group, scaling=scaling)
    flops = 2 * 2 * slots * total_rows * (window + fresh) * width
    cost = pl.CostEstimate(
        flops=flops,
        transcendentals=slots * total_rows * (window + fresh),
        bytes_accessed=2 * (2 * padded_queries.size + 2 * cache_keys.size + 2 * fresh_keys.size),
    )
    return pl.pallas_call(
        kernel,
        grid_spec=pltpu.PrefetchScalarGridSpec(
            num_scalar_prefetch=1,
            grid=(slots, total_rows // rows),
            in_specs=[
                pl.BlockSpec((1, rows, width), lambda s, r, n: (s, r, 0)),
                pl.BlockSpec((1, width, window), lambda s, r, n: (s, 0, 0)),
                pl.BlockSpec((1, width, window), lambda s, r, n: (s, 0, 0)),
                pl.BlockSpec((1, fresh, width), lambda s, r, n: (s, 0, 0)),
                pl.BlockSpec((1, fresh, width), lambda s, r, n: (s, 0, 0)),
            ],
            out_specs=pl.BlockSpec((1, rows, width), lambda s, r, n: (s, r, 0)),
        ),
        out_shape=jax.ShapeDtypeStruct((slots, total_rows, width), jnp.bfloat16),
        compiler_params=pltpu.CompilerParams(dimension_semantics=("arbitrary", "arbitrary")),
        cost_estimate=cost,
    )(lengths, padded_queries, cache_keys, cache_values, fresh_keys, fresh_values)


def feed_forward(rows_in, mlp_gain, w_gate, w_up, w_down):
    normed_rows = rms_norm(rows_in, mlp_gain).astype(jnp.bfloat16)
    block_rows = tok_gather(normed_rows, 0)
    gate_part = jnp.dot(block_rows, w_gate, preferred_element_type=jnp.float32)
    up_part = jnp.dot(block_rows, w_up, preferred_element_type=jnp.float32)
    activated = (jax.nn.silu(gate_part) * up_part).astype(jnp.bfloat16)
    summed = tok_reduce(
        jnp.dot(activated, w_down, preferred_element_type=jnp.float32), 0
    )
    return (rows_in.astype(jnp.float32) + summed).astype(jnp.bfloat16)


def swap_tok(part):
    return lax.ppermute(part, "tok", [(0, 1), (1, 0)])


def in_token_order(own, other):
    me = lax.axis_index("tok")
    first = jnp.where(me == 0, own, other)
    second = jnp.where(me == 0, other, own)
    return jnp.concatenate([first, second], axis=0)


def split_token_order(whole):
    me = lax.axis_index("tok")
    half = whole.shape[0] // 2
    low, high = whole[:half], whole[half:]
    return jnp.where(me == 0, low, high), jnp.where(me == 0, high, low)


def local(
    hidden_in,
    cache_keys,
    stored_cache_values,
    cache_lengths,
    live_slots,
    attn_gain,
    w_query,
    key_weight,
    value_weight,
    w_out,
    mlp_gain,
    w_gate,
    w_up,
    w_down,
):
    slots, quarter, model_width = hidden_in.shape
    new_rows = quarter * lax.axis_size("tok")
    query_width = w_query.shape[1]
    key_width = key_weight.shape[1]
    query_heads = query_width // HEAD_DIM
    key_heads = key_width // HEAD_DIM
    query_group_count = query_heads // key_heads
    head_rows = new_rows * query_group_count
    alive_slots = lax.dynamic_slice_in_dim(live_slots, lax.axis_index("req") * slots, slots)
    empty_value_rows = jnp.zeros((), jnp.bfloat16)
    keys_t = jnp.swapaxes(cache_keys, 1, 2)
    values_t = jnp.swapaxes(stored_cache_values, 1, 2)

    def hidden_half(block):
        gate_part = jnp.dot(block, w_gate, preferred_element_type=jnp.float32)
        up_part = jnp.dot(block, w_up, preferred_element_type=jnp.float32)
        activated = (jax.nn.silu(gate_part) * up_part).astype(jnp.bfloat16)
        return jnp.dot(activated, w_down, preferred_element_type=jnp.float32)

    outs, keys_out, values_out = [], [], []
    for slot in range(slots):
        alive = alive_slots[slot] > 0
        length = cache_lengths[slot]
        tokens = hidden_in[slot]
        normed = rms_norm(tokens, attn_gain).astype(jnp.bfloat16)
        block_rows = in_token_order(normed, swap_tok(normed))
        queries = jnp.dot(block_rows, w_query, preferred_element_type=jnp.float32)
        fresh_keys = jnp.dot(block_rows, key_weight, preferred_element_type=jnp.float32)
        fresh_values = jnp.dot(block_rows, value_weight, preferred_element_type=jnp.float32)
        token_positions = length + jnp.arange(new_rows, dtype=jnp.int32)
        queries = apply_rotary(
            queries.reshape(new_rows, query_heads, HEAD_DIM), token_positions
        ).astype(jnp.bfloat16)
        fresh_keys = apply_rotary(
            fresh_keys.reshape(new_rows, key_heads, HEAD_DIM), token_positions
        ).astype(jnp.bfloat16).reshape(new_rows, key_width)
        fresh_values = fresh_values.astype(jnp.bfloat16)
        keys_out.append(jnp.where(alive, fresh_keys, empty_value_rows))
        values_out.append(jnp.where(alive, fresh_values, empty_value_rows))
        padded = []
        for head in range(key_heads):
            head_queries = queries[
                :, head * query_group_count : (head + 1) * query_group_count, :
            ].reshape(head_rows, HEAD_DIM)
            padded.append(
                jnp.pad(
                    head_queries,
                    ((0, 0), (head * HEAD_DIM, (key_heads - 1 - head) * HEAD_DIM)),
                )
            )
        attended_rows = attend_all(
            jnp.concatenate(padded, axis=0)[None],
            keys_t[slot : slot + 1],
            values_t[slot : slot + 1],
            fresh_keys[None],
            fresh_values[None],
            cache_lengths[slot : slot + 1],
            query_group_count,
        )[0]
        attended = jnp.concatenate(
            [
                attended_rows[
                    h * head_rows : (h + 1) * head_rows, h * HEAD_DIM : (h + 1) * HEAD_DIM
                ].reshape(new_rows, query_group_count * HEAD_DIM)
                for h in range(key_heads)
            ],
            axis=1,
        )
        projected = jnp.dot(attended, w_out, preferred_element_type=jnp.float32)
        own_proj, other_proj = split_token_order(projected)
        received = swap_tok(other_proj.astype(jnp.bfloat16)).astype(jnp.float32)
        residual = (tokens.astype(jnp.float32) + (own_proj + received)).astype(jnp.bfloat16)
        mlp_in = rms_norm(residual, mlp_gain).astype(jnp.bfloat16)
        both = hidden_half(jnp.concatenate([mlp_in, swap_tok(mlp_in)], axis=0))
        own_part = both[:quarter]
        partner_part = swap_tok(both[quarter:].astype(jnp.bfloat16)).astype(jnp.float32)
        completed = (
            residual.astype(jnp.float32) + (own_part + partner_part)
        ).astype(jnp.bfloat16)
        outs.append(jnp.where(alive, completed, empty_value_rows))
    return (jnp.stack(outs), jnp.stack(keys_out), jnp.stack(values_out))


def solution(mesh):
    return jax.shard_map(
        local,
        mesh=mesh,
        in_specs=(
            P("req", "tok", None),
            P("req", None, "tok"),
            P("req", None, "tok"),
            P("req"),
            P(),
            P(),
            P(None, "tok"),
            P(None, "tok"),
            P(None, "tok"),
            P("tok", None),
            P(),
            P(None, "tok"),
            P(None, "tok"),
            P("tok", None),
        ),
        out_specs=(P("req", "tok", None), P("req", None, "tok"), P("req", None, "tok")),
        check_vma=False,
    )
```

```python
import functools

import jax
import jax.numpy as jnp
from jax import lax
from jax.experimental import pallas as pl
from jax.experimental.pallas import tpu as pltpu
from jax.sharding import PartitionSpec as P

HEAD_DIM = 80


EPSILON = 1e-05
ROPE_BASE = 10000.0


def rms_norm(values, norm_gain):
    widened = values.astype(jnp.float32)
    mean_square = jnp.mean(widened * widened, axis=-1, keepdims=True)
    return widened * lax.rsqrt(mean_square + EPSILON) * norm_gain


def tok_gather(part, axis):
    me = lax.axis_index("tok")
    other = lax.ppermute(part, "tok", [(0, 1), (1, 0)])
    first = jnp.where(me == 0, part, other)
    second = jnp.where(me == 0, other, part)
    return jnp.concatenate([first, second], axis=axis)


def tok_reduce(whole, axis):
    me = lax.axis_index("tok")
    half = whole.shape[axis] // 2
    low = lax.slice_in_dim(whole, 0, half, axis=axis)
    high = lax.slice_in_dim(whole, half, 2 * half, axis=axis)
    keep = jnp.where(me == 0, low, high)
    send = jnp.where(me == 0, high, low).astype(jnp.bfloat16)
    other = lax.ppermute(send, "tok", [(0, 1), (1, 0)])
    return keep + other.astype(jnp.float32)


def apply_rotary(values, token_positions):
    full_width = values.shape[-1]
    half_width = full_width // 2
    inverse = ROPE_BASE ** (-(jnp.arange(half_width, dtype=jnp.float32) * 2.0) / full_width)
    angles = token_positions.astype(jnp.float32)[..., None] * inverse
    cosine = jnp.cos(angles)[..., None, :]
    sine_part = jnp.sin(angles)[..., None, :]
    first_half = values[..., :half_width]
    second_half = values[..., half_width:]
    return jnp.concatenate(
        [
            first_half * cosine - second_half * sine_part,
            second_half * cosine + first_half * sine_part,
        ],
        axis=-1,
    )


NEG = -jnp.inf
KEY_BLOCK = 1024
LOG2E = 1.4426950408889634


def attention_kernel(len_ref, q_ref, kc_ref, vc_ref, kn_ref, vn_ref, o_ref, *, group, scaling):
    slot = pl.program_id(0)
    rows = q_ref.shape[1]
    window = kc_ref.shape[2]
    fresh = kn_ref.shape[1]
    heads_rows = fresh * group
    blocks = window // KEY_BLOCK
    length = len_ref[slot]
    q = q_ref[0]
    row = pl.program_id(1) * rows + lax.broadcasted_iota(jnp.int32, (rows, 1), 0)
    token = (row % heads_rows) // group
    transposed = (((1,), (1,)), ((), ()))
    scores = lax.dot_general(q, kn_ref[0], transposed, preferred_element_type=jnp.float32) * scaling
    fresh_pos = lax.broadcasted_iota(jnp.int32, (1, fresh), 1)
    scores = jnp.where(fresh_pos <= token, scores, NEG)
    top = jnp.max(scores, axis=1, keepdims=True)
    raised = jnp.exp2(scores - top)
    mass = jnp.sum(raised, axis=1, keepdims=True)
    total = jnp.dot(raised.astype(jnp.bfloat16), vn_ref[0], preferred_element_type=jnp.float32)
    lowest = window - length
    first_block = jnp.minimum(jnp.maximum(lowest, 0) // KEY_BLOCK, blocks - 1)

    def step(block, carry, masked):
        top, mass, total = carry
        begin = pl.multiple_of(block * KEY_BLOCK, KEY_BLOCK)
        keys = kc_ref[0, :, pl.ds(begin, KEY_BLOCK)]
        values = vc_ref[0, :, pl.ds(begin, KEY_BLOCK)]
        scores = jnp.dot(q, keys, preferred_element_type=jnp.float32) * scaling
        if masked:
            key_pos = begin + lax.broadcasted_iota(jnp.int32, (1, KEY_BLOCK), 1)
            visible = (key_pos >= lowest) & (key_pos > token)
            scores = jnp.where(visible, scores, NEG)
        raised_top = jnp.maximum(top, jnp.max(scores, axis=1, keepdims=True))
        shrink = jnp.exp2(top - raised_top)
        raised = jnp.exp2(scores - raised_top)
        mass = mass * shrink + jnp.sum(raised, axis=1, keepdims=True)
        total = total * shrink + lax.dot_general(
            raised.astype(jnp.bfloat16),
            values,
            transposed,
            preferred_element_type=jnp.float32,
        )
        return raised_top, mass, total

    carry = step(first_block, (top, mass, total), True)
    top, mass, total = lax.fori_loop(
        first_block + 1, blocks, lambda b, c: step(b, c, False), carry
    )
    o_ref[0] = (total / mass).astype(o_ref.dtype)


def attend_all(padded_queries, cache_keys, cache_values, fresh_keys, fresh_values, lengths, group, rows=2048):
    slots, total_rows, width = padded_queries.shape
    window = cache_keys.shape[2]
    fresh = fresh_keys.shape[1]

    scaling = HEAD_DIM ** (-0.5) * LOG2E
    kernel = functools.partial(attention_kernel, group=group, scaling=scaling)
    flops = 2 * 2 * slots * total_rows * (window + fresh) * width
    cost = pl.CostEstimate(
        flops=flops,
        transcendentals=slots * total_rows * (window + fresh),
        bytes_accessed=2 * (2 * padded_queries.size + 2 * cache_keys.size + 2 * fresh_keys.size),
    )
    return pl.pallas_call(
        kernel,
        grid_spec=pltpu.PrefetchScalarGridSpec(
            num_scalar_prefetch=1,
            grid=(slots, total_rows // rows),
            in_specs=[
                pl.BlockSpec((1, rows, width), lambda s, r, n: (s, r, 0)),
                pl.BlockSpec((1, width, window), lambda s, r, n: (s, 0, 0)),
                pl.BlockSpec((1, width, window), lambda s, r, n: (s, 0, 0)),
                pl.BlockSpec((1, fresh, width), lambda s, r, n: (s, 0, 0)),
                pl.BlockSpec((1, fresh, width), lambda s, r, n: (s, 0, 0)),
            ],
            out_specs=pl.BlockSpec((1, rows, width), lambda s, r, n: (s, r, 0)),
        ),
        out_shape=jax.ShapeDtypeStruct((slots, total_rows, width), jnp.bfloat16),
        compiler_params=pltpu.CompilerParams(dimension_semantics=("arbitrary", "arbitrary")),
        cost_estimate=cost,
    )(lengths, padded_queries, cache_keys, cache_values, fresh_keys, fresh_values)


def feed_forward(rows_in, mlp_gain, w_gate, w_up, w_down):
    normed_rows = rms_norm(rows_in, mlp_gain).astype(jnp.bfloat16)
    block_rows = tok_gather(normed_rows, 0)
    gate_part = jnp.dot(block_rows, w_gate, preferred_element_type=jnp.float32)
    up_part = jnp.dot(block_rows, w_up, preferred_element_type=jnp.float32)
    activated = (jax.nn.silu(gate_part) * up_part).astype(jnp.bfloat16)
    summed = tok_reduce(
        jnp.dot(activated, w_down, preferred_element_type=jnp.float32), 0
    )
    return (rows_in.astype(jnp.float32) + summed).astype(jnp.bfloat16)


def swap_tok(part):
    return lax.ppermute(part, "tok", [(0, 1), (1, 0)])


def swap_far(part):
    pairs = []
    for req in range(lax.axis_size("req")):
        for tok in range(2):
            pairs.append((req * 2 + tok, (req ^ 2) * 2 + (1 - tok)))
    return lax.ppermute(part, ("req", "tok"), pairs)


def in_token_order(own, other):
    me = lax.axis_index("tok")
    first = jnp.where(me == 0, own, other)
    second = jnp.where(me == 0, other, own)
    return jnp.concatenate([first, second], axis=0)


def split_token_order(whole):
    me = lax.axis_index("tok")
    half = whole.shape[0] // 2
    low, high = whole[:half], whole[half:]
    return jnp.where(me == 0, low, high), jnp.where(me == 0, high, low)


def local(
    hidden_in,
    cache_keys,
    stored_cache_values,
    cache_lengths,
    live_slots,
    attn_gain,
    w_query,
    key_weight,
    value_weight,
    w_out,
    mlp_gain,
    w_gate,
    w_up,
    w_down,
):
    slots, quarter, model_width = hidden_in.shape
    new_rows = quarter * lax.axis_size("tok")
    query_width = w_query.shape[1]
    key_width = key_weight.shape[1]
    query_heads = query_width // HEAD_DIM
    key_heads = key_width // HEAD_DIM
    query_group_count = query_heads // key_heads
    head_rows = new_rows * query_group_count
    alive_slots = lax.dynamic_slice_in_dim(live_slots, lax.axis_index("req") * slots, slots)
    empty_value_rows = jnp.zeros((), jnp.bfloat16)
    keys_t = jnp.swapaxes(cache_keys, 1, 2)
    values_t = jnp.swapaxes(stored_cache_values, 1, 2)

    def hidden_half(block):
        gate_part = jnp.dot(block, w_gate, preferred_element_type=jnp.float32)
        up_part = jnp.dot(block, w_up, preferred_element_type=jnp.float32)
        activated = (jax.nn.silu(gate_part) * up_part).astype(jnp.bfloat16)
        return jnp.dot(activated, w_down, preferred_element_type=jnp.float32)

    outs, keys_out, values_out = [], [], []
    for slot in range(slots):
        alive = alive_slots[slot] > 0
        length = cache_lengths[slot]
        tokens = hidden_in[slot]
        normed = rms_norm(tokens, attn_gain).astype(jnp.bfloat16)
        block_rows = in_token_order(normed, swap_tok(normed))
        queries = jnp.dot(block_rows, w_query, preferred_element_type=jnp.float32)
        fresh_keys = jnp.dot(block_rows, key_weight, preferred_element_type=jnp.float32)
        fresh_values = jnp.dot(block_rows, value_weight, preferred_element_type=jnp.float32)
        token_positions = length + jnp.arange(new_rows, dtype=jnp.int32)
        queries = apply_rotary(
            queries.reshape(new_rows, query_heads, HEAD_DIM), token_positions
        ).astype(jnp.bfloat16)
        fresh_keys = apply_rotary(
            fresh_keys.reshape(new_rows, key_heads, HEAD_DIM), token_positions
        ).astype(jnp.bfloat16).reshape(new_rows, key_width)
        fresh_values = fresh_values.astype(jnp.bfloat16)
        keys_out.append(jnp.where(alive, fresh_keys, empty_value_rows))
        values_out.append(jnp.where(alive, fresh_values, empty_value_rows))
        padded = []
        for head in range(key_heads):
            head_queries = queries[
                :, head * query_group_count : (head + 1) * query_group_count, :
            ].reshape(head_rows, HEAD_DIM)
            padded.append(
                jnp.pad(
                    head_queries,
                    ((0, 0), (head * HEAD_DIM, (key_heads - 1 - head) * HEAD_DIM)),
                )
            )
        attended_rows = attend_all(
            jnp.concatenate(padded, axis=0)[None],
            keys_t[slot : slot + 1],
            values_t[slot : slot + 1],
            fresh_keys[None],
            fresh_values[None],
            cache_lengths[slot : slot + 1],
            query_group_count,
        )[0]
        attended = jnp.concatenate(
            [
                attended_rows[
                    h * head_rows : (h + 1) * head_rows, h * HEAD_DIM : (h + 1) * HEAD_DIM
                ].reshape(new_rows, query_group_count * HEAD_DIM)
                for h in range(key_heads)
            ],
            axis=1,
        )
        projected = jnp.dot(attended, w_out, preferred_element_type=jnp.float32)
        own_proj, other_proj = split_token_order(projected)
        received = swap_tok(other_proj.astype(jnp.bfloat16)).astype(jnp.float32)
        residual = (tokens.astype(jnp.float32) + (own_proj + received)).astype(jnp.bfloat16)
        mlp_in = rms_norm(residual, mlp_gain).astype(jnp.bfloat16)
        half = quarter // 2
        own_part = hidden_half(mlp_in)
        guest = hidden_half(
            jnp.concatenate([swap_tok(mlp_in[:half]), swap_far(mlp_in[half:])], axis=0)
        ).astype(jnp.bfloat16)
        partner_part = jnp.concatenate(
            [swap_tok(guest[:half]), swap_far(guest[half:])], axis=0
        ).astype(jnp.float32)
        completed = (
            residual.astype(jnp.float32) + (own_part + partner_part)
        ).astype(jnp.bfloat16)
        outs.append(jnp.where(alive, completed, empty_value_rows))
    return (jnp.stack(outs), jnp.stack(keys_out), jnp.stack(values_out))


def solution(mesh):
    return jax.shard_map(
        local,
        mesh=mesh,
        in_specs=(
            P("req", "tok", None),
            P("req", None, "tok"),
            P("req", None, "tok"),
            P("req"),
            P(),
            P(),
            P(None, "tok"),
            P(None, "tok"),
            P(None, "tok"),
            P("tok", None),
            P(),
            P(None, "tok"),
            P(None, "tok"),
            P("tok", None),
        ),
        out_specs=(P("req", "tok", None), P("req", None, "tok"), P("req", None, "tok")),
        check_vma=False,
    )
```

```python
import functools

import jax
import jax.numpy as jnp
from jax import lax
from jax.experimental import pallas as pl
from jax.experimental.pallas import tpu as pltpu
from jax.sharding import PartitionSpec as P

HEAD_DIM = 80


EPSILON = 1e-05
ROPE_BASE = 10000.0


def rms_norm(values, norm_gain):
    widened = values.astype(jnp.float32)
    mean_square = jnp.mean(widened * widened, axis=-1, keepdims=True)
    return widened * lax.rsqrt(mean_square + EPSILON) * norm_gain


def tok_gather(part, axis):
    me = lax.axis_index("tok")
    other = lax.ppermute(part, "tok", [(0, 1), (1, 0)])
    first = jnp.where(me == 0, part, other)
    second = jnp.where(me == 0, other, part)
    return jnp.concatenate([first, second], axis=axis)


def tok_reduce(whole, axis):
    me = lax.axis_index("tok")
    half = whole.shape[axis] // 2
    low = lax.slice_in_dim(whole, 0, half, axis=axis)
    high = lax.slice_in_dim(whole, half, 2 * half, axis=axis)
    keep = jnp.where(me == 0, low, high)
    send = jnp.where(me == 0, high, low).astype(jnp.bfloat16)
    other = lax.ppermute(send, "tok", [(0, 1), (1, 0)])
    return keep + other.astype(jnp.float32)


def apply_rotary(values, token_positions):
    full_width = values.shape[-1]
    half_width = full_width // 2
    inverse = ROPE_BASE ** (-(jnp.arange(half_width, dtype=jnp.float32) * 2.0) / full_width)
    angles = token_positions.astype(jnp.float32)[..., None] * inverse
    cosine = jnp.cos(angles)[..., None, :]
    sine_part = jnp.sin(angles)[..., None, :]
    first_half = values[..., :half_width]
    second_half = values[..., half_width:]
    return jnp.concatenate(
        [
            first_half * cosine - second_half * sine_part,
            second_half * cosine + first_half * sine_part,
        ],
        axis=-1,
    )


NEG = -jnp.inf
KEY_BLOCK = 1024
LOG2E = 1.4426950408889634


def attention_kernel(len_ref, q_ref, kc_ref, vc_ref, kn_ref, vn_ref, o_ref, *, group, scaling):
    slot = pl.program_id(0)
    rows = q_ref.shape[1]
    window = kc_ref.shape[2]
    fresh = kn_ref.shape[1]
    heads_rows = fresh * group
    blocks = window // KEY_BLOCK
    length = len_ref[slot]
    q = q_ref[0]
    row = pl.program_id(1) * rows + lax.broadcasted_iota(jnp.int32, (rows, 1), 0)
    token = (row % heads_rows) // group
    transposed = (((1,), (1,)), ((), ()))
    scores = lax.dot_general(q, kn_ref[0], transposed, preferred_element_type=jnp.float32) * scaling
    fresh_pos = lax.broadcasted_iota(jnp.int32, (1, fresh), 1)
    scores = jnp.where(fresh_pos <= token, scores, NEG)
    top = jnp.max(scores, axis=1, keepdims=True)
    raised = jnp.exp2(scores - top)
    mass = jnp.sum(raised, axis=1, keepdims=True)
    total = jnp.dot(raised.astype(jnp.bfloat16), vn_ref[0], preferred_element_type=jnp.float32)
    lowest = window - length
    first_block = jnp.minimum(jnp.maximum(lowest, 0) // KEY_BLOCK, blocks - 1)

    def step(block, carry, masked):
        top, mass, total = carry
        begin = pl.multiple_of(block * KEY_BLOCK, KEY_BLOCK)
        keys = kc_ref[0, :, pl.ds(begin, KEY_BLOCK)]
        values = vc_ref[0, :, pl.ds(begin, KEY_BLOCK)]
        scores = jnp.dot(q, keys, preferred_element_type=jnp.float32) * scaling
        if masked:
            key_pos = begin + lax.broadcasted_iota(jnp.int32, (1, KEY_BLOCK), 1)
            visible = (key_pos >= lowest) & (key_pos > token)
            scores = jnp.where(visible, scores, NEG)
        raised_top = jnp.maximum(top, jnp.max(scores, axis=1, keepdims=True))
        shrink = jnp.exp2(top - raised_top)
        raised = jnp.exp2(scores - raised_top)
        mass = mass * shrink + jnp.sum(raised, axis=1, keepdims=True)
        total = total * shrink + lax.dot_general(
            raised.astype(jnp.bfloat16),
            values,
            transposed,
            preferred_element_type=jnp.float32,
        )
        return raised_top, mass, total

    carry = step(first_block, (top, mass, total), True)
    top, mass, total = lax.fori_loop(
        first_block + 1, blocks, lambda b, c: step(b, c, False), carry
    )
    o_ref[0] = (total / mass).astype(o_ref.dtype)


def attend_all(padded_queries, cache_keys, cache_values, fresh_keys, fresh_values, lengths, group, rows=2048):
    slots, total_rows, width = padded_queries.shape
    window = cache_keys.shape[2]
    fresh = fresh_keys.shape[1]

    scaling = HEAD_DIM ** (-0.5) * LOG2E
    kernel = functools.partial(attention_kernel, group=group, scaling=scaling)
    flops = 2 * 2 * slots * total_rows * (window + fresh) * width
    cost = pl.CostEstimate(
        flops=flops,
        transcendentals=slots * total_rows * (window + fresh),
        bytes_accessed=2 * (2 * padded_queries.size + 2 * cache_keys.size + 2 * fresh_keys.size),
    )
    return pl.pallas_call(
        kernel,
        grid_spec=pltpu.PrefetchScalarGridSpec(
            num_scalar_prefetch=1,
            grid=(slots, total_rows // rows),
            in_specs=[
                pl.BlockSpec((1, rows, width), lambda s, r, n: (s, r, 0)),
                pl.BlockSpec((1, width, window), lambda s, r, n: (s, 0, 0)),
                pl.BlockSpec((1, width, window), lambda s, r, n: (s, 0, 0)),
                pl.BlockSpec((1, fresh, width), lambda s, r, n: (s, 0, 0)),
                pl.BlockSpec((1, fresh, width), lambda s, r, n: (s, 0, 0)),
            ],
            out_specs=pl.BlockSpec((1, rows, width), lambda s, r, n: (s, r, 0)),
        ),
        out_shape=jax.ShapeDtypeStruct((slots, total_rows, width), jnp.bfloat16),
        compiler_params=pltpu.CompilerParams(dimension_semantics=("arbitrary", "arbitrary")),
        cost_estimate=cost,
    )(lengths, padded_queries, cache_keys, cache_values, fresh_keys, fresh_values)


def feed_forward(rows_in, mlp_gain, w_gate, w_up, w_down):
    normed_rows = rms_norm(rows_in, mlp_gain).astype(jnp.bfloat16)
    block_rows = tok_gather(normed_rows, 0)
    gate_part = jnp.dot(block_rows, w_gate, preferred_element_type=jnp.float32)
    up_part = jnp.dot(block_rows, w_up, preferred_element_type=jnp.float32)
    activated = (jax.nn.silu(gate_part) * up_part).astype(jnp.bfloat16)
    summed = tok_reduce(
        jnp.dot(activated, w_down, preferred_element_type=jnp.float32), 0
    )
    return (rows_in.astype(jnp.float32) + summed).astype(jnp.bfloat16)


def swap_tok(part):
    return lax.ppermute(part, "tok", [(0, 1), (1, 0)])


def swap_far(part):
    pairs = []
    for req in range(lax.axis_size("req")):
        for tok in range(2):
            pairs.append((req * 2 + tok, (req ^ 2) * 2 + (1 - tok)))
    return lax.ppermute(part, ("req", "tok"), pairs)


def in_token_order(own, other):
    me = lax.axis_index("tok")
    first = jnp.where(me == 0, own, other)
    second = jnp.where(me == 0, other, own)
    return jnp.concatenate([first, second], axis=0)


def split_token_order(whole):
    me = lax.axis_index("tok")
    half = whole.shape[0] // 2
    low, high = whole[:half], whole[half:]
    return jnp.where(me == 0, low, high), jnp.where(me == 0, high, low)


def local(
    hidden_in,
    cache_keys,
    stored_cache_values,
    cache_lengths,
    live_slots,
    attn_gain,
    w_query,
    key_weight,
    value_weight,
    w_out,
    mlp_gain,
    w_gate,
    w_up,
    w_down,
):
    slots, quarter, model_width = hidden_in.shape
    new_rows = quarter * lax.axis_size("tok")
    query_width = w_query.shape[1]
    key_width = key_weight.shape[1]
    query_heads = query_width // HEAD_DIM
    key_heads = key_width // HEAD_DIM
    query_group_count = query_heads // key_heads
    head_rows = new_rows * query_group_count
    alive_slots = lax.dynamic_slice_in_dim(live_slots, lax.axis_index("req") * slots, slots)
    empty_value_rows = jnp.zeros((), jnp.bfloat16)
    keys_t = jnp.swapaxes(cache_keys, 1, 2)
    values_t = jnp.swapaxes(stored_cache_values, 1, 2)

    def hidden_half(block):
        gate_part = jnp.dot(block, w_gate, preferred_element_type=jnp.float32)
        up_part = jnp.dot(block, w_up, preferred_element_type=jnp.float32)
        activated = (jax.nn.silu(gate_part) * up_part).astype(jnp.bfloat16)
        return jnp.dot(activated, w_down, preferred_element_type=jnp.float32)

    outs, keys_out, values_out = [], [], []
    for slot in range(slots):
        alive = alive_slots[slot] > 0
        length = cache_lengths[slot]
        tokens = hidden_in[slot]
        normed = rms_norm(tokens, attn_gain).astype(jnp.bfloat16)
        block_rows = in_token_order(normed, swap_tok(normed))
        queries = jnp.dot(block_rows, w_query, preferred_element_type=jnp.float32)
        fresh_keys = jnp.dot(block_rows, key_weight, preferred_element_type=jnp.float32)
        fresh_values = jnp.dot(block_rows, value_weight, preferred_element_type=jnp.float32)
        token_positions = length + jnp.arange(new_rows, dtype=jnp.int32)
        queries = apply_rotary(
            queries.reshape(new_rows, query_heads, HEAD_DIM), token_positions
        ).astype(jnp.bfloat16)
        fresh_keys = apply_rotary(
            fresh_keys.reshape(new_rows, key_heads, HEAD_DIM), token_positions
        ).astype(jnp.bfloat16).reshape(new_rows, key_width)
        fresh_values = fresh_values.astype(jnp.bfloat16)
        keys_out.append(jnp.where(alive, fresh_keys, empty_value_rows))
        values_out.append(jnp.where(alive, fresh_values, empty_value_rows))
        padded = []
        for head in range(key_heads):
            head_queries = queries[
                :, head * query_group_count : (head + 1) * query_group_count, :
            ].reshape(head_rows, HEAD_DIM)
            padded.append(
                jnp.pad(
                    head_queries,
                    ((0, 0), (head * HEAD_DIM, (key_heads - 1 - head) * HEAD_DIM)),
                )
            )
        attended_rows = attend_all(
            jnp.concatenate(padded, axis=0)[None],
            keys_t[slot : slot + 1],
            values_t[slot : slot + 1],
            fresh_keys[None],
            fresh_values[None],
            cache_lengths[slot : slot + 1],
            query_group_count,
        )[0]
        attended = jnp.concatenate(
            [
                attended_rows[
                    h * head_rows : (h + 1) * head_rows, h * HEAD_DIM : (h + 1) * HEAD_DIM
                ].reshape(new_rows, query_group_count * HEAD_DIM)
                for h in range(key_heads)
            ],
            axis=1,
        )
        projected = jnp.dot(attended, w_out, preferred_element_type=jnp.float32)
        own_proj, other_proj = split_token_order(projected)
        received = swap_tok(other_proj.astype(jnp.bfloat16))
        if slot > 0:
            earlier_own, received = lax.optimization_barrier((earlier_own, received))
        received = received.astype(jnp.float32)
        residual = (tokens.astype(jnp.float32) + (own_proj + received)).astype(jnp.bfloat16)
        mlp_in = rms_norm(residual, mlp_gain).astype(jnp.bfloat16)
        half = quarter // 2
        own_part = hidden_half(mlp_in)
        earlier_own = own_part
        guest = hidden_half(
            jnp.concatenate([swap_tok(mlp_in[:half]), swap_far(mlp_in[half:])], axis=0)
        ).astype(jnp.bfloat16)
        partner_part = jnp.concatenate(
            [swap_tok(guest[:half]), swap_far(guest[half:])], axis=0
        ).astype(jnp.float32)
        completed = (
            residual.astype(jnp.float32) + (own_part + partner_part)
        ).astype(jnp.bfloat16)
        outs.append(jnp.where(alive, completed, empty_value_rows))
    return (jnp.stack(outs), jnp.stack(keys_out), jnp.stack(values_out))


def solution(mesh):
    return jax.shard_map(
        local,
        mesh=mesh,
        in_specs=(
            P("req", "tok", None),
            P("req", None, "tok"),
            P("req", None, "tok"),
            P("req"),
            P(),
            P(),
            P(None, "tok"),
            P(None, "tok"),
            P(None, "tok"),
            P("tok", None),
            P(),
            P(None, "tok"),
            P(None, "tok"),
            P("tok", None),
        ),
        out_specs=(P("req", "tok", None), P("req", None, "tok"), P("req", None, "tok")),
        check_vma=False,
    )
```

```python
import functools

import jax
import jax.numpy as jnp
from jax import lax
from jax.experimental import pallas as pl
from jax.experimental.pallas import tpu as pltpu
from jax.sharding import PartitionSpec as P

HEAD_DIM = 80


EPSILON = 1e-05
ROPE_BASE = 10000.0


def rms_norm(values, norm_gain):
    widened = values.astype(jnp.float32)
    mean_square = jnp.mean(widened * widened, axis=-1, keepdims=True)
    return widened * lax.rsqrt(mean_square + EPSILON) * norm_gain


def tok_gather(part, axis):
    me = lax.axis_index("tok")
    other = lax.ppermute(part, "tok", [(0, 1), (1, 0)])
    first = jnp.where(me == 0, part, other)
    second = jnp.where(me == 0, other, part)
    return jnp.concatenate([first, second], axis=axis)


def tok_reduce(whole, axis):
    me = lax.axis_index("tok")
    half = whole.shape[axis] // 2
    low = lax.slice_in_dim(whole, 0, half, axis=axis)
    high = lax.slice_in_dim(whole, half, 2 * half, axis=axis)
    keep = jnp.where(me == 0, low, high)
    send = jnp.where(me == 0, high, low).astype(jnp.bfloat16)
    other = lax.ppermute(send, "tok", [(0, 1), (1, 0)])
    return keep + other.astype(jnp.float32)


def apply_rotary(values, token_positions):
    full_width = values.shape[-1]
    half_width = full_width // 2
    inverse = ROPE_BASE ** (-(jnp.arange(half_width, dtype=jnp.float32) * 2.0) / full_width)
    angles = token_positions.astype(jnp.float32)[..., None] * inverse
    cosine = jnp.cos(angles)[..., None, :]
    sine_part = jnp.sin(angles)[..., None, :]
    first_half = values[..., :half_width]
    second_half = values[..., half_width:]
    return jnp.concatenate(
        [
            first_half * cosine - second_half * sine_part,
            second_half * cosine + first_half * sine_part,
        ],
        axis=-1,
    )


NEG = -jnp.inf
KEY_BLOCK = 1024
LOG2E = 1.4426950408889634


def attention_kernel(
    len_ref, q_ref, kc_ref, vc_ref, kn_ref, vn_ref, o_ref, *, group, scaling, first_slot
):
    slot = first_slot + pl.program_id(0)
    rows = q_ref.shape[1]
    window = kc_ref.shape[2]
    fresh = kn_ref.shape[1]
    heads_rows = fresh * group
    blocks = window // KEY_BLOCK
    length = len_ref[slot]
    q = q_ref[0]
    row = pl.program_id(1) * rows + lax.broadcasted_iota(jnp.int32, (rows, 1), 0)
    token = (row % heads_rows) // group
    transposed = (((1,), (1,)), ((), ()))
    scores = lax.dot_general(q, kn_ref[0], transposed, preferred_element_type=jnp.float32) * scaling
    fresh_pos = lax.broadcasted_iota(jnp.int32, (1, fresh), 1)
    scores = jnp.where(fresh_pos <= token, scores, NEG)
    top = jnp.max(scores, axis=1, keepdims=True)
    raised = jnp.exp2(scores - top)
    mass = jnp.sum(raised, axis=1, keepdims=True)
    total = jnp.dot(raised.astype(jnp.bfloat16), vn_ref[0], preferred_element_type=jnp.float32)
    lowest = window - length
    first_block = jnp.minimum(jnp.maximum(lowest, 0) // KEY_BLOCK, blocks - 1)

    def step(block, carry, masked):
        top, mass, total = carry
        begin = pl.multiple_of(block * KEY_BLOCK, KEY_BLOCK)
        keys = kc_ref[0, :, pl.ds(begin, KEY_BLOCK)]
        values = vc_ref[0, :, pl.ds(begin, KEY_BLOCK)]
        scores = jnp.dot(q, keys, preferred_element_type=jnp.float32) * scaling
        if masked:
            key_pos = begin + lax.broadcasted_iota(jnp.int32, (1, KEY_BLOCK), 1)
            visible = (key_pos >= lowest) & (key_pos > token)
            scores = jnp.where(visible, scores, NEG)
        raised_top = jnp.maximum(top, jnp.max(scores, axis=1, keepdims=True))
        shrink = jnp.exp2(top - raised_top)
        raised = jnp.exp2(scores - raised_top)
        mass = mass * shrink + jnp.sum(raised, axis=1, keepdims=True)
        total = total * shrink + lax.dot_general(
            raised.astype(jnp.bfloat16),
            values,
            transposed,
            preferred_element_type=jnp.float32,
        )
        return raised_top, mass, total

    carry = step(first_block, (top, mass, total), True)
    top, mass, total = lax.fori_loop(
        first_block + 1, blocks, lambda b, c: step(b, c, False), carry
    )
    o_ref[0] = (total / mass).astype(o_ref.dtype)


def attend_all(
    padded_queries, cache_keys, cache_values, fresh_keys, fresh_values, lengths, group,
    rows=2048, first_slot=0,
):
    slots, total_rows, width = padded_queries.shape
    window = cache_keys.shape[2]
    fresh = fresh_keys.shape[1]

    scaling = HEAD_DIM ** (-0.5) * LOG2E
    kernel = functools.partial(
        attention_kernel, group=group, scaling=scaling, first_slot=first_slot
    )
    flops = 2 * 2 * slots * total_rows * (window + fresh) * width
    cost = pl.CostEstimate(
        flops=flops,
        transcendentals=slots * total_rows * (window + fresh),
        bytes_accessed=2 * (2 * padded_queries.size + 2 * slots * width * window + 2 * fresh_keys.size),
    )
    return pl.pallas_call(
        kernel,
        grid_spec=pltpu.PrefetchScalarGridSpec(
            num_scalar_prefetch=1,
            grid=(slots, total_rows // rows),
            in_specs=[
                pl.BlockSpec((1, rows, width), lambda s, r, n: (s, r, 0)),
                pl.BlockSpec((1, width, window), lambda s, r, n: (first_slot + s, 0, 0)),
                pl.BlockSpec((1, width, window), lambda s, r, n: (first_slot + s, 0, 0)),
                pl.BlockSpec((1, fresh, width), lambda s, r, n: (s, 0, 0)),
                pl.BlockSpec((1, fresh, width), lambda s, r, n: (s, 0, 0)),
            ],
            out_specs=pl.BlockSpec((1, rows, width), lambda s, r, n: (s, r, 0)),
        ),
        out_shape=jax.ShapeDtypeStruct((slots, total_rows, width), jnp.bfloat16),
        compiler_params=pltpu.CompilerParams(dimension_semantics=("arbitrary", "arbitrary")),
        cost_estimate=cost,
    )(lengths, padded_queries, cache_keys, cache_values, fresh_keys, fresh_values)


def feed_forward(rows_in, mlp_gain, w_gate, w_up, w_down):
    normed_rows = rms_norm(rows_in, mlp_gain).astype(jnp.bfloat16)
    block_rows = tok_gather(normed_rows, 0)
    gate_part = jnp.dot(block_rows, w_gate, preferred_element_type=jnp.float32)
    up_part = jnp.dot(block_rows, w_up, preferred_element_type=jnp.float32)
    activated = (jax.nn.silu(gate_part) * up_part).astype(jnp.bfloat16)
    summed = tok_reduce(
        jnp.dot(activated, w_down, preferred_element_type=jnp.float32), 0
    )
    return (rows_in.astype(jnp.float32) + summed).astype(jnp.bfloat16)


def swap_tok(part):
    return lax.ppermute(part, "tok", [(0, 1), (1, 0)])


def swap_far(part):
    pairs = []
    for req in range(lax.axis_size("req")):
        for tok in range(2):
            pairs.append((req * 2 + tok, (req ^ 2) * 2 + (1 - tok)))
    return lax.ppermute(part, ("req", "tok"), pairs)


def in_token_order(own, other):
    me = lax.axis_index("tok")
    first = jnp.where(me == 0, own, other)
    second = jnp.where(me == 0, other, own)
    return jnp.concatenate([first, second], axis=0)


def split_token_order(whole):
    me = lax.axis_index("tok")
    half = whole.shape[0] // 2
    low, high = whole[:half], whole[half:]
    return jnp.where(me == 0, low, high), jnp.where(me == 0, high, low)


def local(
    hidden_in,
    cache_keys,
    stored_cache_values,
    cache_lengths,
    live_slots,
    attn_gain,
    w_query,
    key_weight,
    value_weight,
    w_out,
    mlp_gain,
    w_gate,
    w_up,
    w_down,
):
    slots, quarter, model_width = hidden_in.shape
    new_rows = quarter * lax.axis_size("tok")
    query_width = w_query.shape[1]
    key_width = key_weight.shape[1]
    query_heads = query_width // HEAD_DIM
    key_heads = key_width // HEAD_DIM
    query_group_count = query_heads // key_heads
    head_rows = new_rows * query_group_count
    alive_slots = lax.dynamic_slice_in_dim(live_slots, lax.axis_index("req") * slots, slots)
    empty_value_rows = jnp.zeros((), jnp.bfloat16)
    keys_t = jnp.swapaxes(cache_keys, 1, 2)
    values_t = jnp.swapaxes(stored_cache_values, 1, 2)

    def hidden_half(block):
        gate_part = jnp.dot(block, w_gate, preferred_element_type=jnp.float32)
        up_part = jnp.dot(block, w_up, preferred_element_type=jnp.float32)
        activated = (jax.nn.silu(gate_part) * up_part).astype(jnp.bfloat16)
        return jnp.dot(activated, w_down, preferred_element_type=jnp.float32)

    outs, keys_out, values_out = [], [], []
    for slot in range(slots):
        alive = alive_slots[slot] > 0
        length = cache_lengths[slot]
        tokens = hidden_in[slot]
        normed = rms_norm(tokens, attn_gain).astype(jnp.bfloat16)
        block_rows = in_token_order(normed, swap_tok(normed))
        queries = jnp.dot(block_rows, w_query, preferred_element_type=jnp.float32)
        fresh_keys = jnp.dot(block_rows, key_weight, preferred_element_type=jnp.float32)
        fresh_values = jnp.dot(block_rows, value_weight, preferred_element_type=jnp.float32)
        token_positions = length + jnp.arange(new_rows, dtype=jnp.int32)
        queries = apply_rotary(
            queries.reshape(new_rows, query_heads, HEAD_DIM), token_positions
        ).astype(jnp.bfloat16)
        fresh_keys = apply_rotary(
            fresh_keys.reshape(new_rows, key_heads, HEAD_DIM), token_positions
        ).astype(jnp.bfloat16).reshape(new_rows, key_width)
        fresh_values = fresh_values.astype(jnp.bfloat16)
        keys_out.append(jnp.where(alive, fresh_keys, empty_value_rows))
        values_out.append(jnp.where(alive, fresh_values, empty_value_rows))
        padded = []
        for head in range(key_heads):
            head_queries = queries[
                :, head * query_group_count : (head + 1) * query_group_count, :
            ].reshape(head_rows, HEAD_DIM)
            padded.append(
                jnp.pad(
                    head_queries,
                    ((0, 0), (head * HEAD_DIM, (key_heads - 1 - head) * HEAD_DIM)),
                )
            )
        attended_rows = attend_all(
            jnp.concatenate(padded, axis=0)[None],
            keys_t,
            values_t,
            fresh_keys[None],
            fresh_values[None],
            cache_lengths,
            query_group_count,
            first_slot=slot,
        )[0]
        attended = jnp.concatenate(
            [
                attended_rows[
                    h * head_rows : (h + 1) * head_rows, h * HEAD_DIM : (h + 1) * HEAD_DIM
                ].reshape(new_rows, query_group_count * HEAD_DIM)
                for h in range(key_heads)
            ],
            axis=1,
        )
        projected = jnp.dot(attended, w_out, preferred_element_type=jnp.float32)
        own_proj, other_proj = split_token_order(projected)
        received = swap_tok(other_proj.astype(jnp.bfloat16))
        if slot > 0:
            earlier_own, received = lax.optimization_barrier((earlier_own, received))
        received = received.astype(jnp.float32)
        residual = (tokens.astype(jnp.float32) + (own_proj + received)).astype(jnp.bfloat16)
        mlp_in = rms_norm(residual, mlp_gain).astype(jnp.bfloat16)
        half = quarter // 2
        own_part = hidden_half(mlp_in)
        earlier_own = own_part
        guest = hidden_half(
            jnp.concatenate([swap_tok(mlp_in[:half]), swap_far(mlp_in[half:])], axis=0)
        ).astype(jnp.bfloat16)
        partner_part = jnp.concatenate(
            [swap_tok(guest[:half]), swap_far(guest[half:])], axis=0
        ).astype(jnp.float32)
        completed = (
            residual.astype(jnp.float32) + (own_part + partner_part)
        ).astype(jnp.bfloat16)
        outs.append(jnp.where(alive, completed, empty_value_rows))
    return (jnp.stack(outs), jnp.stack(keys_out), jnp.stack(values_out))


def solution(mesh):
    return jax.shard_map(
        local,
        mesh=mesh,
        in_specs=(
            P("req", "tok", None),
            P("req", None, "tok"),
            P("req", None, "tok"),
            P("req"),
            P(),
            P(),
            P(None, "tok"),
            P(None, "tok"),
            P(None, "tok"),
            P("tok", None),
            P(),
            P(None, "tok"),
            P(None, "tok"),
            P("tok", None),
        ),
        out_specs=(P("req", "tok", None), P("req", None, "tok"), P("req", None, "tok")),
        check_vma=False,
    )
```
